256 devices in a mesh: shell: 4 (over x_lo, core), tile: 64 (over z, x_hi, y).
Axes of the slice: x: 4 (x_hi: 2, x_lo: 2; x = x_hi * 2 + x_lo), y: 4, z: 8, core: 2. Of those that a mesh axis runs over, the one named last changes fastest.
Arguments:
- latent: float32 [64, 2048, 512], P('shell', 'tile'), may hold values from -5 to 5
- shell_sigma: float32 [64], P('shell'), may hold values from 0.15 to 0.6
- lens_weight: float32 [5, 64], P(None, 'shell'), may hold values from 0 to 0.5
- shear_kernel: bfloat16 [2, 33, 33], replicated, may hold values from -0.1875 to 0.1875
- star_mask: int32 [2048, 512], P('tile', 'shell'), may hold values 0 or 1
- gal_pix: int32 [16, 4096, 128], P('shell', 'tile'), may hold values from 0 to 4095
- gal_bin: int32 [16, 4096, 128], P('shell', 'tile'), may hold values from 0 to 4
- gal_shape: float32 [2, 16, 4096, 128], P(None, 'shell', 'tile'), may hold values from -3 to 3
- gal_weight: float32 [16, 4096, 128], P('shell', 'tile'), may hold values from 0.5 to 4
- gal_counts: int32 [16, 4096], P('shell', 'tile'), may hold values from 0 to 128, as said below
Outputs:
- grad_field: float32 [64, 2048, 512], P('shell', 'tile')
The draws below stay inside these ranges and needn't reach their ends.
Inputs may be any that keep to these rules, and one draw needn't show every extreme that they name: Bucket (i, j) of the galaxy arrays holds galaxies for the tile j mod 64 and the column block i mod 4, in its first gal_counts[i, j] slots; in every draw some destination block receives 128 galaxies from every device, and buckets' loads range from near zero to 128.
All inputs are finite; a program needn't handle non-finite values. No bound on the sum of `star_mask` on one device may be relied on, other than what follows from the above.
Results may differ from the reference program's by a relative error of at most 0.0023.
Values may be sent and summed in bfloat16 or wider, within the bound.
No kernel may reach another device: no remote copies, remote signals or barrier semaphores. Data moves between devices by JAX's collectives and lax.ppermute only.
A program may use at most 64 MiB of HBM per device.

```python
import math
import jax
import jax.numpy as jnp
from jax import lax

SHELLS = 64
NBIN = 5
KER = 33
HALF = 16
ROWS_DEV = 32
COLS_DEV = 128
CAP = 128
NROWS = 2048
WIDTH = 512
N_SHELL = 4
N_TILE = 64


def draw_gal_counts(key, part):
    key_level, key_jitter, key_shell, key_tile = jax.random.split(jax.random.fold_in(key, 17), 4)
    load_level = jax.random.randint(key_level, (N_SHELL, N_TILE), 1, 9)
    base_load = jnp.tile(CAP * load_level // 8, (N_SHELL, N_TILE))
    jitter = jax.random.randint(key_jitter, (N_SHELL * N_SHELL, N_TILE * N_TILE), 0, CAP // 8 + 1)
    counts = jnp.maximum(base_load - jitter, 0)
    full_shell = jax.random.randint(key_shell, (), 0, N_SHELL)
    full_tile = jax.random.randint(key_tile, (), 0, N_TILE)
    dest_shell = lax.broadcasted_iota(jnp.int32, counts.shape, 0) % N_SHELL
    dest_tile = lax.broadcasted_iota(jnp.int32, counts.shape, 1) % N_TILE
    chosen = (dest_shell == full_shell) & (dest_tile == full_tile)
    return jnp.where(chosen, CAP, counts).astype(jnp.int32)


def plant(values, stream_key, low, top_value):
    longest = values.shape.index(max(values.shape))
    spots = []
    for shift in (0, 1):
        where = [jax.random.randint(jax.random.fold_in(stream_key, axis), (), 0, length) for axis, length in enumerate(values.shape)]
        where[longest] = (where[longest] + shift) % values.shape[longest]
        spots.append(tuple(where))
    return values.at[spots[0]].set(low).at[spots[1]].set(top_value)


def block_scale(stream_key, extent, shards, least, top_value):
    factor_of = 1.0
    for axis_at, blocks in shards:
        steps = jax.random.uniform(jax.random.fold_in(jax.random.fold_in(stream_key, 6), axis_at), (blocks,), jnp.float32, least / len(shards), top_value / len(shards))
        factor_of = factor_of * jnp.repeat(jnp.exp(steps), extent[axis_at] // blocks).reshape((-1,) + (1,) * (len(extent) - 1 - axis_at))
    return factor_of


def bell_draw(own_key, shape, spread, bound, shards=(), held_as=jnp.bfloat16):
    entries = jax.random.normal(own_key, shape, jnp.float32) * spread
    if len(shards) > 0:
        entries = block_scale(own_key, shape, shards, -0.22, 0.18) * entries
    return jnp.clip(entries, min=-bound, max=bound).astype(held_as)


def setup_inputs(seed: int = 0) -> dict:
    splits = jax.random.split(jax.random.key(seed), 11)
    latent = bell_draw(splits[0], (SHELLS, NROWS, WIDTH), 1.0, 5.0, ((0, 4), (1, 64)), jnp.float32)
    shell_sigma = jnp.clip(jnp.exp(math.log(0.6) - 1.3862944 * jax.random.uniform(splits[1], (SHELLS,), jnp.float32) ** block_scale(splits[1], (SHELLS,), ((0, 4),), -0.2, 0.2)), 0.15, 0.6)
    lens_weight = jnp.clip(0.5 * jax.random.uniform(splits[2], (NBIN, SHELLS), jnp.float32) ** block_scale(splits[2], (NBIN, SHELLS), ((1, 4),), -0.2, 0.2), 0.0, 0.5)
    shear_kernel = bell_draw(splits[3], (2, KER, KER), (KER * KER) ** -0.5, 0.1875)
    star_mask = plant((jax.random.randint(splits[4], (NROWS, WIDTH), 0, 8) < 7).astype(jnp.int32), jax.random.fold_in(splits[4], 1), 0, 1)
    gal_pix = plant(jax.random.randint(splits[5], (N_SHELL * N_SHELL, N_TILE * N_TILE, CAP), 0, ROWS_DEV * COLS_DEV), jax.random.fold_in(splits[5], 1), 0, (ROWS_DEV * COLS_DEV) - 1).astype(jnp.int32)
    gal_bin = plant(jax.random.randint(splits[6], (N_SHELL * N_SHELL, N_TILE * N_TILE, CAP), 0, NBIN), jax.random.fold_in(splits[6], 1), 0, NBIN - 1).astype(jnp.int32)
    gal_shape = bell_draw(splits[7], (2, N_SHELL * N_SHELL, N_TILE * N_TILE, CAP), 0.5, 3.0, ((1, 4), (2, 64)), jnp.float32)
    gal_weight = jnp.clip(jnp.exp(math.log(4.0) - 2.0794415 * jax.random.uniform(splits[8], (N_SHELL * N_SHELL, N_TILE * N_TILE, CAP), jnp.float32) ** block_scale(splits[8], (N_SHELL * N_SHELL, N_TILE * N_TILE, CAP), ((0, 4), (1, 64)), -0.2, 0.2)), 0.5, 4.0)
    gal_counts = draw_gal_counts(jax.random.fold_in(splits[10], 71), 0)
    return dict(latent=latent, shell_sigma=shell_sigma, lens_weight=lens_weight, shear_kernel=shear_kernel, star_mask=star_mask, gal_pix=gal_pix, gal_bin=gal_bin, gal_shape=gal_shape, gal_weight=gal_weight, gal_counts=gal_counts)


def correlate(maps, kernel):
    height = maps.shape[1]
    width = maps.shape[2]
    padded = jnp.pad(maps, ((0, 0), (HALF, HALF), (HALF, HALF)))
    kernel_pad = jnp.pad(kernel, ((0, height + 2 * HALF - KER), (0, width + 2 * HALF - KER)))
    spectrum = jnp.fft.rfft2(padded) * jnp.conj(jnp.fft.rfft2(kernel_pad))[None]
    result = jnp.fft.irfft2(spectrum, s=(height + 2 * HALF, width + 2 * HALF))
    return result[:, :height, :width]


def reference(latent, shell_sigma, lens_weight, shear_kernel, star_mask, gal_pix, gal_bin, gal_shape, gal_weight, gal_counts):
    sigma = shell_sigma[:, None, None]
    growth = jnp.exp(sigma * latent - 0.5 * sigma * sigma)
    bin_map = jnp.einsum("bs,srw->brw", lens_weight, growth - 1.0, precision=lax.Precision.HIGHEST).astype(jnp.bfloat16)
    kernel = shear_kernel.astype(jnp.float32)
    bin_float = bin_map.astype(jnp.float32)
    shear = jnp.stack([correlate(bin_float, kernel[0]), correlate(bin_float, kernel[1])])
    shell_rows = gal_pix.shape[0]
    tile_rows = gal_pix.shape[1]
    dest_shell = (jnp.arange(shell_rows, dtype=jnp.int32) % N_SHELL).astype(jnp.int32)[:, None, None]
    dest_tile = (jnp.arange(tile_rows, dtype=jnp.int32) % N_TILE).astype(jnp.int32)[None, :, None]
    pixel_row = dest_tile * ROWS_DEV + gal_pix // COLS_DEV
    pixel_col = dest_shell * COLS_DEV + gal_pix % COLS_DEV
    target = ((gal_bin * NROWS + pixel_row) * WIDTH + pixel_col).reshape(-1).astype(jnp.int32)
    usable = (jnp.arange(CAP, dtype=jnp.int32)[None, None, :] < gal_counts[:, :, None]).reshape(-1)
    shear_flat = shear.reshape(2, -1)
    predicted = shear_flat[:, target]
    weights = jnp.where(usable, gal_weight.reshape(-1), 0.0)
    residual = weights * (predicted - gal_shape.reshape(2, -1))
    summed = jnp.zeros_like(shear_flat).at[:, target].add(residual)
    summed = summed.reshape(2, NBIN, NROWS, WIDTH)
    shear_grad = (summed * star_mask.astype(jnp.float32)).astype(jnp.bfloat16).astype(jnp.float32)
    flipped = jnp.flip(kernel, (1, 2))
    bin_grad = correlate(shear_grad[0], flipped[0]) + correlate(shear_grad[1], flipped[1])
    mixed = jnp.einsum("bs,brw->srw", lens_weight, bin_grad, precision=lax.Precision.HIGHEST)
    return sigma * growth * mixed
```

```python
import functools

import jax
import jax.numpy as jnp
from jax import lax
from jax.experimental import pallas as pl
from jax.experimental.pallas import tpu as pltpu
from jax.sharding import PartitionSpec as P

NBIN = 5
KER = 33
HALF = 16
CHUNK = 1024


def extended(block, sides, width):
    for axis, dim in sides:
        count = lax.axis_size(axis)
        forward = [(i, i + 1) for i in range(count - 1)]
        backward = [(target, source) for source, target in forward]
        low = lax.ppermute(
            lax.slice_in_dim(block, block.shape[dim] - width, None, axis=dim), axis, forward
        )
        high = lax.ppermute(lax.slice_in_dim(block, 0, width, axis=dim), axis, backward)
        block = jnp.concatenate([low, block, high], axis=dim)
    return block


def build_bands(kernel, columns):
    span = columns + KER - 1
    grid_shape = (KER, span, columns)
    lagged = lax.broadcasted_iota(jnp.int32, grid_shape, 1) - lax.broadcasted_iota(
        jnp.int32, grid_shape, 2
    )
    onehot = (lagged == lax.broadcasted_iota(jnp.int32, grid_shape, 0)).astype(jnp.bfloat16)
    bands = jnp.einsum("kdv,vjc->kdjc", kernel, onehot, preferred_element_type=jnp.float32)
    return bands.astype(jnp.bfloat16)


def stacked_rows(padded, height):
    return jnp.stack([padded[..., offset : offset + height, :] for offset in range(KER)], axis=-3)


def split_bf16(value):
    high = value.astype(jnp.bfloat16)
    low = (value - high.astype(jnp.float32)).astype(jnp.bfloat16)
    return high, low


def scatter_kernel(rows, columns, packet_ref, out_ref):
    out_ref[...] = jnp.zeros_like(out_ref)
    steps = packet_ref.shape[1] // CHUNK

    def body(step, carry):
        start = pl.multiple_of(step * CHUNK, CHUNK)
        block = packet_ref[:, pl.ds(start, CHUNK)]
        code = block[0:1].astype(jnp.int32)
        row_of = code >> 7
        col_of = code & (columns - 1)
        row_hot = (lax.broadcasted_iota(jnp.int32, (rows, CHUNK), 0) == row_of).astype(
            jnp.bfloat16
        )
        col_hot = lax.broadcasted_iota(jnp.int32, (columns, CHUNK), 0) == col_of
        zero = jnp.zeros((columns, CHUNK), jnp.bfloat16)
        parts = []
        for field in (1, 2, 3):
            for piece in split_bf16(block[field : field + 1]):
                parts.append(jnp.where(col_hot, jnp.broadcast_to(piece, (columns, CHUNK)), zero))
        spread = jnp.concatenate(parts, axis=0)
        out_ref[...] += lax.dot_general(
            row_hot,
            spread,
            (((1,), (1,)), ((), ())),
            preferred_element_type=jnp.float32,
        )
        return carry

    lax.fori_loop(0, steps, body, 0)


def deposit_sums(packet, rows, columns):
    count = packet.shape[1]
    flops = 2 * rows * 6 * columns * count
    return pl.pallas_call(
        functools.partial(scatter_kernel, rows, columns),
        out_shape=jax.ShapeDtypeStruct((rows, 6 * columns), jnp.float32),
        in_specs=[pl.BlockSpec(memory_space=pltpu.VMEM)],
        out_specs=pl.BlockSpec(memory_space=pltpu.VMEM),
        cost_estimate=pl.CostEstimate(
            flops=flops, bytes_accessed=packet.size * 4 + rows * 6 * columns * 4, transcendentals=0
        ),
    )(packet)


def per_device(
    latent,
    shell_sigma,
    lens_weight,
    shear_kernel,
    star_mask,
    gal_pix,
    gal_bin,
    gal_shape,
    gal_weight,
    gal_counts,
):
    height = latent.shape[1]
    width = latent.shape[2]
    shell_count = lax.axis_size("shell")
    columns = width // shell_count
    pixels = height * columns

    slot_index = lax.broadcasted_iota(jnp.int32, gal_pix.shape, 2)
    usable = slot_index < gal_counts[:, :, None]
    codes = jnp.where(usable, gal_bin * pixels + gal_pix, 0).astype(jnp.float32)
    weights = jnp.where(usable, gal_weight, 0.0)
    packet = jnp.concatenate(
        [codes[None], weights[None], weights[None] * gal_shape], axis=0
    )
    arrived = lax.all_to_all(
        lax.all_to_all(packet, "shell", split_axis=1, concat_axis=1, tiled=True),
        "tile",
        split_axis=2,
        concat_axis=2,
        tiled=True,
    )
    sums = deposit_sums(arrived.reshape(4, -1), NBIN * height, columns)
    sums = sums.reshape(NBIN, height, 6, columns)
    sums = sums[:, :, 0::2] + sums[:, :, 1::2]
    weight_sum = sums[:, :, 0]
    shape_sum = jnp.stack([sums[:, :, 1], sums[:, :, 2]])

    sigma = shell_sigma[:, None, None]
    growth = jnp.exp(sigma * latent - 0.5 * sigma * sigma)
    partial_bins = jnp.einsum(
        "bs,srw->brw",
        lens_weight,
        growth - 1.0,
        precision=lax.Precision.HIGHEST,
        preferred_element_type=jnp.float32,
    )
    bin_map = lax.psum_scatter(partial_bins, "shell", scatter_dimension=2, tiled=True).astype(
        jnp.bfloat16
    )
    padded = extended(bin_map, (("shell", 2), ("tile", 1)), HALF)
    forward_bands = build_bands(shear_kernel, columns)
    shear = jnp.einsum(
        "bdrj,kdjc->kbrc",
        stacked_rows(padded, height),
        forward_bands,
        preferred_element_type=jnp.float32,
    )
    shear_grad = shear * weight_sum[None] - shape_sum
    masked = (shear_grad * star_mask.astype(jnp.float32)).astype(jnp.bfloat16)
    rims = extended(masked, (("shell", 3), ("tile", 2)), HALF)
    back_bands = build_bands(jnp.flip(shear_kernel, (1, 2)), columns)
    bin_grad = jnp.einsum(
        "kbdrj,kdjc->brc",
        stacked_rows(rims, height),
        back_bands,
        preferred_element_type=jnp.float32,
    )
    full_grad = lax.all_gather(bin_grad, "shell", axis=2, tiled=True)
    mixed = jnp.einsum(
        "bs,brw->srw",
        lens_weight,
        full_grad,
        precision=lax.Precision.HIGHEST,
        preferred_element_type=jnp.float32,
    )
    return sigma * growth * mixed


def solution(mesh):
    return jax.shard_map(
        per_device,
        mesh=mesh,
        in_specs=(
            P("shell", "tile", None),
            P("shell"),
            P(None, "shell"),
            P(),
            P("tile", "shell"),
            P("shell", "tile", None),
            P("shell", "tile", None),
            P(None, "shell", "tile", None),
            P("shell", "tile", None),
            P("shell", "tile"),
        ),
        out_specs=P("shell", "tile", None),
        check_vma=False,
    )
```

```python
import functools

import jax
import jax.numpy as jnp
from jax import lax
from jax.experimental import pallas as pl
from jax.experimental.pallas import tpu as pltpu
from jax.sharding import PartitionSpec as P

NBIN = 5
KER = 33
HALF = 16
CHUNK = 1024


def extended(block, sides, width):
    for axis, dim in sides:
        count = lax.axis_size(axis)
        forward = [(i, i + 1) for i in range(count - 1)]
        backward = [(target, source) for source, target in forward]
        low = lax.ppermute(
            lax.slice_in_dim(block, block.shape[dim] - width, None, axis=dim), axis, forward
        )
        high = lax.ppermute(lax.slice_in_dim(block, 0, width, axis=dim), axis, backward)
        block = jnp.concatenate([low, block, high], axis=dim)
    return block


def build_bands(kernel, columns):
    span = columns + KER - 1
    grid_shape = (KER, span, columns)
    lagged = lax.broadcasted_iota(jnp.int32, grid_shape, 1) - lax.broadcasted_iota(
        jnp.int32, grid_shape, 2
    )
    onehot = (lagged == lax.broadcasted_iota(jnp.int32, grid_shape, 0)).astype(jnp.bfloat16)
    bands = jnp.einsum("kdv,vjc->kdjc", kernel, onehot, preferred_element_type=jnp.float32)
    return bands.astype(jnp.bfloat16)


def stacked_rows(padded, height):
    return jnp.stack([padded[..., offset : offset + height, :] for offset in range(KER)], axis=-3)


def split_bf16(value):
    high = value.astype(jnp.bfloat16)
    low = (value - high.astype(jnp.float32)).astype(jnp.bfloat16)
    return high, low


def scatter_kernel(rows, columns, packet_ref, out_ref, acc_ref):
    acc_ref[...] = jnp.zeros_like(acc_ref)
    steps = packet_ref.shape[1] // CHUNK

    def body(step, carry):
        start = pl.multiple_of(step * CHUNK, CHUNK)
        block = packet_ref[:, pl.ds(start, CHUNK)]
        code = block[0:1].astype(jnp.int32)
        row_of = code >> 7
        col_of = code & (columns - 1)
        row_hot = (lax.broadcasted_iota(jnp.int32, (rows, CHUNK), 0) == row_of).astype(
            jnp.bfloat16
        )
        col_hot = lax.broadcasted_iota(jnp.int32, (columns, CHUNK), 0) == col_of
        zero = jnp.zeros((columns, CHUNK), jnp.bfloat16)
        pieces = [split_bf16(block[field : field + 1]) for field in (1, 2, 3)]
        parts = [
            jnp.where(col_hot, jnp.broadcast_to(piece[half], (columns, CHUNK)), zero)
            for half in (0, 1)
            for piece in pieces
        ]
        spread = jnp.concatenate(parts, axis=0)
        acc_ref[...] += lax.dot_general(
            row_hot,
            spread,
            (((1,), (1,)), ((), ())),
            preferred_element_type=jnp.float32,
        )
        return carry

    lax.fori_loop(0, steps, body, 0)
    for field in range(3):
        out_ref[field] = (
            acc_ref[:, field * columns : (field + 1) * columns]
            + acc_ref[:, (field + 3) * columns : (field + 4) * columns]
        )


def deposit_sums(packet, rows, columns):
    count = packet.shape[1]
    flops = 2 * rows * 6 * columns * count
    return pl.pallas_call(
        functools.partial(scatter_kernel, rows, columns),
        out_shape=jax.ShapeDtypeStruct((3, rows, columns), jnp.float32),
        in_specs=[pl.BlockSpec(memory_space=pltpu.VMEM)],
        out_specs=pl.BlockSpec(memory_space=pltpu.VMEM),
        scratch_shapes=[pltpu.VMEM((rows, 6 * columns), jnp.float32)],
        cost_estimate=pl.CostEstimate(
            flops=flops, bytes_accessed=packet.size * 4 + rows * 3 * columns * 4, transcendentals=0
        ),
    )(packet)


def per_device(
    latent,
    shell_sigma,
    lens_weight,
    shear_kernel,
    star_mask,
    gal_pix,
    gal_bin,
    gal_shape,
    gal_weight,
    gal_counts,
):
    height = latent.shape[1]
    width = latent.shape[2]
    shell_count = lax.axis_size("shell")
    columns = width // shell_count
    pixels = height * columns

    slot_index = lax.broadcasted_iota(jnp.int32, gal_pix.shape, 2)
    usable = slot_index < gal_counts[:, :, None]
    codes = jnp.where(usable, gal_bin * pixels + gal_pix, 0).astype(jnp.float32)
    weights = jnp.where(usable, gal_weight, 0.0)
    packet = jnp.concatenate(
        [codes[None], weights[None], weights[None] * gal_shape], axis=0
    )
    arrived = lax.all_to_all(
        lax.all_to_all(packet, "shell", split_axis=1, concat_axis=1, tiled=True),
        "tile",
        split_axis=2,
        concat_axis=2,
        tiled=True,
    )
    sums = deposit_sums(arrived.reshape(4, -1), NBIN * height, columns)
    sums = sums.reshape(3, NBIN, height, columns)
    weight_sum = sums[0]
    shape_sum = sums[1:]

    sigma = shell_sigma[:, None, None]
    growth = jnp.exp(sigma * latent - 0.5 * sigma * sigma)
    partial_bins = jnp.einsum(
        "bs,srw->brw",
        lens_weight,
        growth - 1.0,
        precision=lax.Precision.HIGHEST,
        preferred_element_type=jnp.float32,
    )
    wide = jnp.pad(partial_bins, ((0, 0), (0, 0), (HALF, HALF)))
    windows = jnp.stack(
        [wide[:, :, owner * columns : owner * columns + columns + 2 * HALF] for owner in range(shell_count)]
    )
    gathered = lax.all_to_all(windows, "shell", split_axis=0, concat_axis=0, tiled=True)
    bin_map = jnp.sum(gathered, axis=0).astype(jnp.bfloat16)
    padded = extended(bin_map, (("tile", 1),), HALF)
    forward_bands = build_bands(shear_kernel, columns)
    shear = jnp.einsum(
        "bdrj,kdjc->kbrc",
        stacked_rows(padded, height),
        forward_bands,
        preferred_element_type=jnp.float32,
    )
    shear_grad = shear * weight_sum[None] - shape_sum
    masked = (shear_grad * star_mask.astype(jnp.float32)).astype(jnp.bfloat16)
    rims = extended(masked, (("shell", 3), ("tile", 2)), HALF)
    back_bands = build_bands(jnp.flip(shear_kernel, (1, 2)), columns)
    bin_grad = jnp.einsum(
        "kbdrj,kdjc->brc",
        stacked_rows(rims, height),
        back_bands,
        preferred_element_type=jnp.float32,
    )
    full_grad = lax.all_gather(bin_grad, "shell", axis=2, tiled=True)
    mixed = jnp.einsum(
        "bs,brw->srw",
        lens_weight,
        full_grad,
        precision=lax.Precision.HIGHEST,
        preferred_element_type=jnp.float32,
    )
    return sigma * growth * mixed


def solution(mesh):
    return jax.shard_map(
        per_device,
        mesh=mesh,
        in_specs=(
            P("shell", "tile", None),
            P("shell"),
            P(None, "shell"),
            P(),
            P("tile", "shell"),
            P("shell", "tile", None),
            P("shell", "tile", None),
            P(None, "shell", "tile", None),
            P("shell", "tile", None),
            P("shell", "tile"),
        ),
        out_specs=P("shell", "tile", None),
        check_vma=False,
    )
```

```python
import functools

import jax
import jax.numpy as jnp
from jax import lax
from jax.experimental import pallas as pl
from jax.experimental.pallas import tpu as pltpu
from jax.sharding import PartitionSpec as P

NBIN = 5
KER = 33
HALF = 16
CHUNK = 1024


def extended(block, sides, width):
    for axis, dim in sides:
        count = lax.axis_size(axis)
        forward = [(i, i + 1) for i in range(count - 1)]
        backward = [(target, source) for source, target in forward]
        low = lax.ppermute(
            lax.slice_in_dim(block, block.shape[dim] - width, None, axis=dim), axis, forward
        )
        high = lax.ppermute(lax.slice_in_dim(block, 0, width, axis=dim), axis, backward)
        block = jnp.concatenate([low, block, high], axis=dim)
    return block


def build_bands(kernel, columns):
    span = columns + KER - 1
    grid_shape = (KER, span, columns)
    lagged = lax.broadcasted_iota(jnp.int32, grid_shape, 1) - lax.broadcasted_iota(
        jnp.int32, grid_shape, 2
    )
    onehot = (lagged == lax.broadcasted_iota(jnp.int32, grid_shape, 0)).astype(jnp.bfloat16)
    bands = jnp.einsum("kdv,vjc->kdjc", kernel, onehot, preferred_element_type=jnp.float32)
    return bands.astype(jnp.bfloat16)


def stacked_rows(padded, height):
    return jnp.stack([padded[..., offset : offset + height, :] for offset in range(KER)], axis=-3)


def split_bf16(value):
    high = value.astype(jnp.bfloat16)
    low = (value - high.astype(jnp.float32)).astype(jnp.bfloat16)
    return high, low


def scatter_kernel(rows, columns, packet_ref, out_ref, acc_ref):
    acc_ref[...] = jnp.zeros_like(acc_ref)
    steps = packet_ref.shape[1] // CHUNK

    def body(step, carry):
        start = pl.multiple_of(step * CHUNK, CHUNK)
        block = packet_ref[:, pl.ds(start, CHUNK)]
        code = block[0:1].astype(jnp.int32)
        row_of = code >> 7
        col_of = code & (columns - 1)
        row_hot = (lax.broadcasted_iota(jnp.int32, (rows, CHUNK), 0) == row_of).astype(
            jnp.bfloat16
        )
        col_hot = lax.broadcasted_iota(jnp.int32, (columns, CHUNK), 0) == col_of
        zero = jnp.zeros((columns, CHUNK), jnp.bfloat16)
        pieces = [split_bf16(block[field : field + 1]) for field in (1, 2, 3)]
        parts = [
            jnp.where(col_hot, jnp.broadcast_to(piece[half], (columns, CHUNK)), zero)
            for half in (0, 1)
            for piece in pieces
        ]
        spread = jnp.concatenate(parts, axis=0)
        acc_ref[...] += lax.dot_general(
            row_hot,
            spread,
            (((1,), (1,)), ((), ())),
            preferred_element_type=jnp.float32,
        )
        return carry

    lax.fori_loop(0, steps, body, 0)
    for field in range(3):
        out_ref[field] = (
            acc_ref[:, field * columns : (field + 1) * columns]
            + acc_ref[:, (field + 3) * columns : (field + 4) * columns]
        )


def deposit_sums(packet, rows, columns):
    count = packet.shape[1]
    flops = 2 * rows * 6 * columns * count
    return pl.pallas_call(
        functools.partial(scatter_kernel, rows, columns),
        out_shape=jax.ShapeDtypeStruct((3, rows, columns), jnp.float32),
        in_specs=[pl.BlockSpec(memory_space=pltpu.VMEM)],
        out_specs=pl.BlockSpec(memory_space=pltpu.VMEM),
        scratch_shapes=[pltpu.VMEM((rows, 6 * columns), jnp.float32)],
        cost_estimate=pl.CostEstimate(
            flops=flops, bytes_accessed=packet.size * 4 + rows * 3 * columns * 4, transcendentals=0
        ),
    )(packet)


def per_device(
    latent,
    shell_sigma,
    lens_weight,
    shear_kernel,
    star_mask,
    gal_pix,
    gal_bin,
    gal_shape,
    gal_weight,
    gal_counts,
):
    height = latent.shape[1]
    width = latent.shape[2]
    shell_count = lax.axis_size("shell")
    columns = width // shell_count
    pixels = height * columns

    slot_index = lax.broadcasted_iota(jnp.int32, gal_pix.shape, 2)
    usable = slot_index < gal_counts[:, :, None]
    codes = jnp.where(usable, gal_bin * pixels + gal_pix, 0).astype(jnp.float32)
    weights = jnp.where(usable, gal_weight, 0.0)
    packet = jnp.concatenate(
        [codes[None], weights[None], weights[None] * gal_shape], axis=0
    )
    devices = packet.shape[1] * packet.shape[2]
    arrived = lax.all_to_all(
        packet.reshape(4, devices, -1), ("shell", "tile"), split_axis=1, concat_axis=1, tiled=True
    )
    sums = deposit_sums(arrived.reshape(4, -1), NBIN * height, columns)
    sums = sums.reshape(3, NBIN, height, columns)
    weight_sum = sums[0]
    shape_sum = sums[1:]

    sigma = shell_sigma[:, None, None]
    growth = jnp.exp(sigma * latent - 0.5 * sigma * sigma)
    partial_bins = jnp.einsum(
        "bs,srw->brw",
        lens_weight,
        growth - 1.0,
        precision=lax.Precision.HIGHEST,
        preferred_element_type=jnp.float32,
    )
    wide = jnp.pad(partial_bins, ((0, 0), (0, 0), (HALF, HALF)))
    windows = jnp.stack(
        [wide[:, :, owner * columns : owner * columns + columns + 2 * HALF] for owner in range(shell_count)]
    )
    gathered = lax.all_to_all(windows, "shell", split_axis=0, concat_axis=0, tiled=True)
    bin_map = jnp.sum(gathered, axis=0).astype(jnp.bfloat16)
    padded = extended(bin_map, (("tile", 1),), HALF)
    forward_bands = build_bands(shear_kernel, columns)
    shear = jnp.einsum(
        "bdrj,kdjc->kbrc",
        stacked_rows(padded, height),
        forward_bands,
        preferred_element_type=jnp.float32,
    )
    shear_grad = shear * weight_sum[None] - shape_sum
    masked = (shear_grad * star_mask.astype(jnp.float32)).astype(jnp.bfloat16)
    rims = extended(masked, (("shell", 3), ("tile", 2)), HALF)
    back_bands = build_bands(jnp.flip(shear_kernel, (1, 2)), columns)
    bin_grad = jnp.einsum(
        "kbdrj,kdjc->brc",
        stacked_rows(rims, height),
        back_bands,
        preferred_element_type=jnp.float32,
    )
    full_grad = lax.all_gather(bin_grad, "shell", axis=2, tiled=True)
    mixed = jnp.einsum(
        "bs,brw->srw",
        lens_weight,
        full_grad,
        precision=lax.Precision.HIGHEST,
        preferred_element_type=jnp.float32,
    )
    return sigma * growth * mixed


def solution(mesh):
    return jax.shard_map(
        per_device,
        mesh=mesh,
        in_specs=(
            P("shell", "tile", None),
            P("shell"),
            P(None, "shell"),
            P(),
            P("tile", "shell"),
            P("shell", "tile", None),
            P("shell", "tile", None),
            P(None, "shell", "tile", None),
            P("shell", "tile", None),
            P("shell", "tile"),
        ),
        out_specs=P("shell", "tile", None),
        check_vma=False,
    )
```

```python
import functools

import jax
import jax.numpy as jnp
from jax import lax
from jax.experimental import pallas as pl
from jax.experimental.pallas import tpu as pltpu
from jax.sharding import PartitionSpec as P

NBIN = 5
KER = 33
HALF = 16
CHUNK = 8192


def extended(block, sides, width):
    for axis, dim in sides:
        count = lax.axis_size(axis)
        forward = [(i, i + 1) for i in range(count - 1)]
        backward = [(target, source) for source, target in forward]
        low = lax.ppermute(
            lax.slice_in_dim(block, block.shape[dim] - width, None, axis=dim), axis, forward
        )
        high = lax.ppermute(lax.slice_in_dim(block, 0, width, axis=dim), axis, backward)
        block = jnp.concatenate([low, block, high], axis=dim)
    return block


def build_bands(kernel, columns):
    span = columns + KER - 1
    grid_shape = (KER, span, columns)
    lagged = lax.broadcasted_iota(jnp.int32, grid_shape, 1) - lax.broadcasted_iota(
        jnp.int32, grid_shape, 2
    )
    onehot = (lagged == lax.broadcasted_iota(jnp.int32, grid_shape, 0)).astype(jnp.bfloat16)
    bands = jnp.einsum("kdv,vjc->kdjc", kernel, onehot, preferred_element_type=jnp.float32)
    return bands.astype(jnp.bfloat16)


def stacked_rows(padded, height):
    return jnp.stack([padded[..., offset : offset + height, :] for offset in range(KER)], axis=-3)


def split_bf16(value):
    high = value.astype(jnp.bfloat16)
    low = (value - high.astype(jnp.float32)).astype(jnp.bfloat16)
    return high, low


def scatter_kernel(rows, columns, packet_ref, out_ref, acc_ref):
    acc_ref[...] = jnp.zeros_like(acc_ref)
    steps = packet_ref.shape[1] // CHUNK

    def body(step, carry):
        start = pl.multiple_of(step * CHUNK, CHUNK)
        block = packet_ref[:, pl.ds(start, CHUNK)]
        code = block[0:1].astype(jnp.int32)
        row_of = code >> 7
        col_of = code & (columns - 1)
        row_hot = (lax.broadcasted_iota(jnp.int32, (rows, CHUNK), 0) == row_of).astype(
            jnp.bfloat16
        )
        col_hot = (lax.broadcasted_iota(jnp.int32, (columns, CHUNK), 0) == col_of).astype(
            jnp.bfloat16
        )
        pieces = [split_bf16(block[field : field + 1]) for field in (1, 2, 3)]
        spread = jnp.concatenate(
            [col_hot * piece[half] for half in (0, 1) for piece in pieces], axis=0
        )
        acc_ref[...] += lax.dot_general(
            spread,
            row_hot,
            (((1,), (1,)), ((), ())),
            preferred_element_type=jnp.float32,
        )
        return carry

    lax.fori_loop(0, steps, body, 0)
    for field in range(3):
        out_ref[field] = (
            acc_ref[field * columns : (field + 1) * columns, :]
            + acc_ref[(field + 3) * columns : (field + 4) * columns, :]
        ).T


def deposit_sums(packet, rows, columns):
    count = packet.shape[1]
    flops = 2 * rows * 6 * columns * count
    return pl.pallas_call(
        functools.partial(scatter_kernel, rows, columns),
        out_shape=jax.ShapeDtypeStruct((3, rows, columns), jnp.float32),
        in_specs=[pl.BlockSpec(memory_space=pltpu.VMEM)],
        out_specs=pl.BlockSpec(memory_space=pltpu.VMEM),
        scratch_shapes=[pltpu.VMEM((6 * columns, rows), jnp.float32)],
        cost_estimate=pl.CostEstimate(
            flops=flops, bytes_accessed=packet.size * 4 + rows * 3 * columns * 4, transcendentals=0
        ),
    )(packet)


def per_device(
    latent,
    shell_sigma,
    lens_weight,
    shear_kernel,
    star_mask,
    gal_pix,
    gal_bin,
    gal_shape,
    gal_weight,
    gal_counts,
):
    height = latent.shape[1]
    width = latent.shape[2]
    shell_count = lax.axis_size("shell")
    columns = width // shell_count
    pixels = height * columns

    slot_index = lax.broadcasted_iota(jnp.int32, gal_pix.shape, 2)
    usable = slot_index < gal_counts[:, :, None]
    codes = jnp.where(usable, gal_bin * pixels + gal_pix, 0).astype(jnp.float32)
    weights = jnp.where(usable, gal_weight, 0.0)
    packet = jnp.concatenate(
        [codes[None], weights[None], weights[None] * gal_shape], axis=0
    )
    devices = packet.shape[1] * packet.shape[2]
    arrived = lax.all_to_all(
        packet.reshape(4, devices, -1), ("shell", "tile"), split_axis=1, concat_axis=1, tiled=True
    )
    sums = deposit_sums(arrived.reshape(4, -1), NBIN * height, columns)
    sums = sums.reshape(3, NBIN, height, columns)
    weight_sum = sums[0]
    shape_sum = sums[1:]

    sigma = shell_sigma[:, None, None]
    growth = jnp.exp(sigma * latent - 0.5 * sigma * sigma)
    partial_bins = jnp.einsum(
        "bs,srw->brw",
        lens_weight,
        growth - 1.0,
        precision=lax.Precision.HIGHEST,
        preferred_element_type=jnp.float32,
    )
    wide = jnp.pad(partial_bins, ((0, 0), (0, 0), (HALF, HALF)))
    windows = jnp.stack(
        [wide[:, :, owner * columns : owner * columns + columns + 2 * HALF] for owner in range(shell_count)]
    )
    gathered = lax.all_to_all(windows, "shell", split_axis=0, concat_axis=0, tiled=True)
    bin_map = jnp.sum(gathered, axis=0).astype(jnp.bfloat16)
    padded = extended(bin_map, (("tile", 1),), HALF)
    forward_bands = build_bands(shear_kernel, columns)
    shear = jnp.einsum(
        "bdrj,kdjc->kbrc",
        stacked_rows(padded, height),
        forward_bands,
        preferred_element_type=jnp.float32,
    )
    shear_grad = shear * weight_sum[None] - shape_sum
    masked = (shear_grad * star_mask.astype(jnp.float32)).astype(jnp.bfloat16)
    rims = extended(masked, (("shell", 3), ("tile", 2)), HALF)
    back_bands = build_bands(jnp.flip(shear_kernel, (1, 2)), columns)
    bin_grad = jnp.einsum(
        "kbdrj,kdjc->brc",
        stacked_rows(rims, height),
        back_bands,
        preferred_element_type=jnp.float32,
    )
    full_grad = lax.all_gather(bin_grad, "shell", axis=2, tiled=True)
    mixed = jnp.einsum(
        "bs,brw->srw",
        lens_weight,
        full_grad,
        precision=lax.Precision.HIGHEST,
        preferred_element_type=jnp.float32,
    )
    return sigma * growth * mixed


def solution(mesh):
    return jax.shard_map(
        per_device,
        mesh=mesh,
        in_specs=(
            P("shell", "tile", None),
            P("shell"),
            P(None, "shell"),
            P(),
            P("tile", "shell"),
            P("shell", "tile", None),
            P("shell", "tile", None),
            P(None, "shell", "tile", None),
            P("shell", "tile", None),
            P("shell", "tile"),
        ),
        out_specs=P("shell", "tile", None),
        check_vma=False,
    )
```

```python
import functools

import jax
import jax.numpy as jnp
from jax import lax
from jax.experimental import pallas as pl
from jax.experimental.pallas import tpu as pltpu
from jax.sharding import PartitionSpec as P


NBIN = 5
KER = 33
HALF = 16
CHUNK = 8192


def extended(block, sides, width):
    for axis, dim in sides:
        count = lax.axis_size(axis)
        forward = [(i, i + 1) for i in range(count - 1)]
        backward = [(target, source) for source, target in forward]
        low = lax.ppermute(
            lax.slice_in_dim(block, block.shape[dim] - width, None, axis=dim), axis, forward
        )
        high = lax.ppermute(lax.slice_in_dim(block, 0, width, axis=dim), axis, backward)
        block = jnp.concatenate([low, block, high], axis=dim)
    return block


def build_bands(kernel, columns):
    span = columns + KER - 1
    grid_shape = (KER, span, columns)
    lagged = lax.broadcasted_iota(jnp.int32, grid_shape, 1) - lax.broadcasted_iota(
        jnp.int32, grid_shape, 2
    )
    onehot = (lagged == lax.broadcasted_iota(jnp.int32, grid_shape, 0)).astype(jnp.bfloat16)
    bands = jnp.einsum("kdv,vjc->kdjc", kernel, onehot, preferred_element_type=jnp.float32)
    return bands.astype(jnp.bfloat16)


def stacked_rows(padded, height):
    return jnp.stack([padded[..., offset : offset + height, :] for offset in range(KER)], axis=-3)


def split_bf16(value):
    high = value.astype(jnp.bfloat16)
    low = (value - high.astype(jnp.float32)).astype(jnp.bfloat16)
    return high, low


def scatter_kernel(rows, columns, packet_ref, out_ref, acc_ref):
    acc_ref[...] = jnp.zeros_like(acc_ref)
    steps = packet_ref.shape[1] // CHUNK

    def body(step, carry):
        start = pl.multiple_of(step * CHUNK, CHUNK)
        block = packet_ref[:, pl.ds(start, CHUNK)]
        code = block[0:1].astype(jnp.int32)
        row_of = code >> 7
        col_of = code & (columns - 1)
        row_hot = (lax.broadcasted_iota(jnp.int32, (rows, CHUNK), 0) == row_of).astype(
            jnp.bfloat16
        )
        col_hot = (lax.broadcasted_iota(jnp.int32, (columns, CHUNK), 0) == col_of).astype(
            jnp.bfloat16
        )
        pieces = [split_bf16(block[field : field + 1]) for field in (1, 2, 3)]
        spread = jnp.concatenate(
            [col_hot * piece[half] for half in (0, 1) for piece in pieces], axis=0
        )
        acc_ref[...] += lax.dot_general(
            spread,
            row_hot,
            (((1,), (1,)), ((), ())),
            preferred_element_type=jnp.float32,
        )
        return carry

    lax.fori_loop(0, steps, body, 0)
    for field in range(3):
        out_ref[field] = (
            acc_ref[field * columns : (field + 1) * columns, :]
            + acc_ref[(field + 3) * columns : (field + 4) * columns, :]
        ).T


def deposit_sums(packet, rows, columns):
    count = packet.shape[1]
    flops = 2 * rows * 6 * columns * count
    return pl.pallas_call(
        functools.partial(scatter_kernel, rows, columns),
        out_shape=jax.ShapeDtypeStruct((3, rows, columns), jnp.float32),
        in_specs=[pl.BlockSpec(memory_space=pltpu.VMEM)],
        out_specs=pl.BlockSpec(memory_space=pltpu.VMEM),
        scratch_shapes=[pltpu.VMEM((6 * columns, rows), jnp.float32)],
        cost_estimate=pl.CostEstimate(
            flops=flops, bytes_accessed=packet.size * 4 + rows * 3 * columns * 4, transcendentals=0
        ),
    )(packet)


def correlate_kernel(x_ref, band_ref, out_ref, z_ref):
    bins, span, width = x_ref.shape
    height = out_ref.shape[2]
    x = x_ref[...].reshape(bins * span, width)
    for k in range(band_ref.shape[0]):
        total = jnp.zeros(out_ref.shape[1:], jnp.float32)
        for offset in range(band_ref.shape[1]):
            z_ref[...] = jnp.dot(
                x, band_ref[k, offset], preferred_element_type=jnp.float32
            ).reshape(z_ref.shape)
            total = total + z_ref[:, offset : offset + height, :]
        out_ref[k] = total


def correlate_forward(padded, bands, height):
    bins, span, width = padded.shape
    kinds, offsets, _, columns = bands.shape
    return pl.pallas_call(
        correlate_kernel,
        out_shape=jax.ShapeDtypeStruct((kinds, bins, height, columns), jnp.float32),
        in_specs=[pl.BlockSpec(memory_space=pltpu.VMEM)] * 2,
        out_specs=pl.BlockSpec(memory_space=pltpu.VMEM),
        scratch_shapes=[pltpu.VMEM((bins, span, columns), jnp.float32)],
        cost_estimate=pl.CostEstimate(
            flops=2 * kinds * offsets * bins * span * width * columns,
            bytes_accessed=padded.size * 2 + bands.size * 2 + kinds * bins * height * columns * 4,
            transcendentals=0,
        ),
    )(padded, bands)


def per_device(
    latent,
    shell_sigma,
    lens_weight,
    shear_kernel,
    star_mask,
    gal_pix,
    gal_bin,
    gal_shape,
    gal_weight,
    gal_counts,
):
    height = latent.shape[1]
    width = latent.shape[2]
    shell_count = lax.axis_size("shell")
    columns = width // shell_count
    pixels = height * columns

    slot_index = lax.broadcasted_iota(jnp.int32, gal_pix.shape, 2)
    usable = slot_index < gal_counts[:, :, None]
    codes = jnp.where(usable, gal_bin * pixels + gal_pix, 0).astype(jnp.float32)
    weights = jnp.where(usable, gal_weight, 0.0)
    packet = jnp.concatenate(
        [codes[None], weights[None], weights[None] * gal_shape], axis=0
    )
    devices = packet.shape[1] * packet.shape[2]
    arrived = lax.all_to_all(
        packet.reshape(4, devices, -1), ("shell", "tile"), split_axis=1, concat_axis=1, tiled=True
    )
    sums = deposit_sums(arrived.reshape(4, -1), NBIN * height, columns)
    sums = sums.reshape(3, NBIN, height, columns)
    weight_sum = sums[0]
    shape_sum = sums[1:]

    sigma = shell_sigma[:, None, None]
    growth = jnp.exp(sigma * latent - 0.5 * sigma * sigma)
    partial_bins = jnp.einsum(
        "bs,srw->brw",
        lens_weight,
        growth - 1.0,
        precision=lax.Precision.HIGHEST,
        preferred_element_type=jnp.float32,
    )
    wide = jnp.pad(partial_bins, ((0, 0), (0, 0), (HALF, HALF)))
    windows = jnp.stack(
        [wide[:, :, owner * columns : owner * columns + columns + 2 * HALF] for owner in range(shell_count)]
    )
    gathered = lax.all_to_all(windows, "shell", split_axis=0, concat_axis=0, tiled=True)
    bin_map = jnp.sum(gathered, axis=0).astype(jnp.bfloat16)
    padded = extended(bin_map, (("tile", 1),), HALF)
    forward_bands = build_bands(shear_kernel, columns)
    shear = correlate_forward(padded, forward_bands, height)
    shear_grad = shear * weight_sum[None] - shape_sum
    masked = (shear_grad * star_mask.astype(jnp.float32)).astype(jnp.bfloat16)
    rims = extended(masked, (("shell", 3), ("tile", 2)), HALF)
    back_bands = build_bands(jnp.flip(shear_kernel, (1, 2)), columns)
    bin_grad = jnp.einsum(
        "kbdrj,kdjc->brc",
        stacked_rows(rims, height),
        back_bands,
        preferred_element_type=jnp.float32,
    )
    full_grad = lax.all_gather(bin_grad, "shell", axis=2, tiled=True)
    mixed = jnp.einsum(
        "bs,brw->srw",
        lens_weight,
        full_grad,
        precision=lax.Precision.HIGHEST,
        preferred_element_type=jnp.float32,
    )
    return sigma * growth * mixed


def solution(mesh):
    return jax.shard_map(
        per_device,
        mesh=mesh,
        in_specs=(
            P("shell", "tile", None),
            P("shell"),
            P(None, "shell"),
            P(),
            P("tile", "shell"),
            P("shell", "tile", None),
            P("shell", "tile", None),
            P(None, "shell", "tile", None),
            P("shell", "tile", None),
            P("shell", "tile"),
        ),
        out_specs=P("shell", "tile", None),
        check_vma=False,
    )
```

```python
import functools

import jax
import jax.numpy as jnp
from jax import lax
from jax.experimental import pallas as pl
from jax.experimental.pallas import tpu as pltpu
from jax.sharding import PartitionSpec as P


NBIN = 5
KER = 33
HALF = 16
CHUNK = 8192


def extended(block, sides, width):
    for axis, dim in sides:
        count = lax.axis_size(axis)
        forward = [(i, i + 1) for i in range(count - 1)]
        backward = [(target, source) for source, target in forward]
        low = lax.ppermute(
            lax.slice_in_dim(block, block.shape[dim] - width, None, axis=dim), axis, forward
        )
        high = lax.ppermute(lax.slice_in_dim(block, 0, width, axis=dim), axis, backward)
        block = jnp.concatenate([low, block, high], axis=dim)
    return block


def build_bands(kernel, columns):
    span = columns + KER - 1
    grid_shape = (KER, span, columns)
    lagged = lax.broadcasted_iota(jnp.int32, grid_shape, 1) - lax.broadcasted_iota(
        jnp.int32, grid_shape, 2
    )
    onehot = (lagged == lax.broadcasted_iota(jnp.int32, grid_shape, 0)).astype(jnp.bfloat16)
    bands = jnp.einsum("kdv,vjc->kdjc", kernel, onehot, preferred_element_type=jnp.float32)
    return bands.astype(jnp.bfloat16)


def stacked_rows(padded, height):
    return jnp.stack([padded[..., offset : offset + height, :] for offset in range(KER)], axis=-3)


def split_bf16(value):
    high = value.astype(jnp.bfloat16)
    low = (value - high.astype(jnp.float32)).astype(jnp.bfloat16)
    return high, low


def scatter_kernel(rows, columns, packet_ref, out_ref, acc_ref):
    acc_ref[...] = jnp.zeros_like(acc_ref)
    steps = packet_ref.shape[1] // CHUNK

    def body(step, carry):
        start = pl.multiple_of(step * CHUNK, CHUNK)
        block = packet_ref[:, pl.ds(start, CHUNK)]
        code = block[0:1].astype(jnp.int32)
        row_of = code >> 7
        col_of = code & (columns - 1)
        row_hot = (lax.broadcasted_iota(jnp.int32, (rows, CHUNK), 0) == row_of).astype(
            jnp.bfloat16
        )
        col_hot = (lax.broadcasted_iota(jnp.int32, (columns, CHUNK), 0) == col_of).astype(
            jnp.bfloat16
        )
        pieces = [split_bf16(block[field : field + 1]) for field in (1, 2, 3)]
        spread = jnp.concatenate(
            [col_hot * piece[half] for half in (0, 1) for piece in pieces], axis=0
        )
        acc_ref[...] += lax.dot_general(
            spread,
            row_hot,
            (((1,), (1,)), ((), ())),
            preferred_element_type=jnp.float32,
        )
        return carry

    lax.fori_loop(0, steps, body, 0)
    for field in range(3):
        out_ref[field] = (
            acc_ref[field * columns : (field + 1) * columns, :]
            + acc_ref[(field + 3) * columns : (field + 4) * columns, :]
        ).T


def deposit_sums(packet, rows, columns):
    count = packet.shape[1]
    flops = 2 * rows * 6 * columns * count
    return pl.pallas_call(
        functools.partial(scatter_kernel, rows, columns),
        out_shape=jax.ShapeDtypeStruct((3, rows, columns), jnp.float32),
        in_specs=[pl.BlockSpec(memory_space=pltpu.VMEM)],
        out_specs=pl.BlockSpec(memory_space=pltpu.VMEM),
        scratch_shapes=[pltpu.VMEM((6 * columns, rows), jnp.float32)],
        cost_estimate=pl.CostEstimate(
            flops=flops, bytes_accessed=packet.size * 4 + rows * 3 * columns * 4, transcendentals=0
        ),
    )(packet)


def correlate_kernel(x_ref, band_ref, out_ref, z_ref):
    bins, span, width = x_ref.shape
    height = out_ref.shape[2]
    x = x_ref[...].reshape(bins * span, width)
    for k in range(band_ref.shape[0]):
        total = jnp.zeros(out_ref.shape[1:], jnp.float32)
        for offset in range(band_ref.shape[1]):
            z_ref[...] = jnp.dot(
                x, band_ref[k, offset], preferred_element_type=jnp.float32
            ).reshape(z_ref.shape)
            total = total + z_ref[:, offset : offset + height, :]
        out_ref[k] = total


def correlate_forward(padded, bands, height):
    bins, span, width = padded.shape
    kinds, offsets, _, columns = bands.shape
    return pl.pallas_call(
        correlate_kernel,
        out_shape=jax.ShapeDtypeStruct((kinds, bins, height, columns), jnp.float32),
        in_specs=[pl.BlockSpec(memory_space=pltpu.VMEM)] * 2,
        out_specs=pl.BlockSpec(memory_space=pltpu.VMEM),
        scratch_shapes=[pltpu.VMEM((bins, span, columns), jnp.float32)],
        cost_estimate=pl.CostEstimate(
            flops=2 * kinds * offsets * bins * span * width * columns,
            bytes_accessed=padded.size * 2 + bands.size * 2 + kinds * bins * height * columns * 4,
            transcendentals=0,
        ),
    )(padded, bands)


def per_device(
    latent,
    shell_sigma,
    lens_weight,
    shear_kernel,
    star_mask,
    gal_pix,
    gal_bin,
    gal_shape,
    gal_weight,
    gal_counts,
):
    height = latent.shape[1]
    width = latent.shape[2]
    shell_count = lax.axis_size("shell")
    columns = width // shell_count
    pixels = height * columns

    slot_index = lax.broadcasted_iota(jnp.int32, gal_pix.shape, 2)
    usable = slot_index < gal_counts[:, :, None]
    codes = jnp.where(usable, gal_bin * pixels + gal_pix, 0).astype(jnp.float32)
    weights = jnp.where(usable, gal_weight, 0.0)
    packet = jnp.concatenate(
        [codes[None], weights[None], weights[None] * gal_shape], axis=0
    )
    devices = packet.shape[1] * packet.shape[2]
    arrived = lax.all_to_all(
        packet.reshape(4, devices, -1), ("shell", "tile"), split_axis=1, concat_axis=1, tiled=True
    )
    sums = deposit_sums(arrived.reshape(4, -1), NBIN * height, columns)
    sums = sums.reshape(3, NBIN, height, columns)
    weight_sum = sums[0]
    shape_sum = sums[1:]

    sigma = shell_sigma[:, None, None]
    growth = jnp.exp(sigma * latent - 0.5 * sigma * sigma)
    partial_bins = jnp.einsum(
        "bs,srw->brw",
        lens_weight,
        growth - 1.0,
        precision=lax.Precision.HIGHEST,
        preferred_element_type=jnp.float32,
    )
    wide = jnp.pad(partial_bins, ((0, 0), (0, 0), (HALF, HALF)))
    windows = jnp.stack(
        [wide[:, :, owner * columns : owner * columns + columns + 2 * HALF] for owner in range(shell_count)]
    )
    me = lax.axis_index("shell")
    total = lax.dynamic_index_in_dim(windows, me, 0, keepdims=False)
    for shift in range(1, shell_count):
        outgoing = lax.dynamic_index_in_dim(windows, (me + shift) % shell_count, 0, keepdims=False)
        total = total + lax.ppermute(
            outgoing, "shell", [(i, (i + shift) % shell_count) for i in range(shell_count)]
        )
    bin_map = total.astype(jnp.bfloat16)
    padded = extended(bin_map, (("tile", 1),), HALF)
    forward_bands = build_bands(shear_kernel, columns)
    shear = correlate_forward(padded, forward_bands, height)
    shear_grad = shear * weight_sum[None] - shape_sum
    masked = (shear_grad * star_mask.astype(jnp.float32)).astype(jnp.bfloat16)
    rims = extended(masked, (("shell", 3), ("tile", 2)), HALF)
    back_bands = build_bands(jnp.flip(shear_kernel, (1, 2)), columns)
    bin_grad = jnp.einsum(
        "kbdrj,kdjc->brc",
        stacked_rows(rims, height),
        back_bands,
        preferred_element_type=jnp.float32,
    )
    full_grad = lax.all_gather(bin_grad, "shell", axis=2, tiled=True)
    mixed = jnp.einsum(
        "bs,brw->srw",
        lens_weight,
        full_grad,
        precision=lax.Precision.HIGHEST,
        preferred_element_type=jnp.float32,
    )
    return sigma * growth * mixed


def solution(mesh):
    return jax.shard_map(
        per_device,
        mesh=mesh,
        in_specs=(
            P("shell", "tile", None),
            P("shell"),
            P(None, "shell"),
            P(),
            P("tile", "shell"),
            P("shell", "tile", None),
            P("shell", "tile", None),
            P(None, "shell", "tile", None),
            P("shell", "tile", None),
            P("shell", "tile"),
        ),
        out_specs=P("shell", "tile", None),
        check_vma=False,
    )
```

```python
import functools

import jax
import jax.numpy as jnp
from jax import lax
from jax.experimental import pallas as pl
from jax.experimental.pallas import tpu as pltpu
from jax.sharding import PartitionSpec as P


NBIN = 5
KER = 33
HALF = 16
CHUNK = 8192


def extended(block, sides, width):
    for axis, dim in sides:
        count = lax.axis_size(axis)
        forward = [(i, i + 1) for i in range(count - 1)]
        backward = [(target, source) for source, target in forward]
        low = lax.ppermute(
            lax.slice_in_dim(block, block.shape[dim] - width, None, axis=dim), axis, forward
        )
        high = lax.ppermute(lax.slice_in_dim(block, 0, width, axis=dim), axis, backward)
        block = jnp.concatenate([low, block, high], axis=dim)
    return block


def build_bands(kernel, columns):
    span = columns + KER - 1
    grid_shape = (KER, span, columns)
    lagged = lax.broadcasted_iota(jnp.int32, grid_shape, 1) - lax.broadcasted_iota(
        jnp.int32, grid_shape, 2
    )
    onehot = (lagged == lax.broadcasted_iota(jnp.int32, grid_shape, 0)).astype(jnp.bfloat16)
    bands = jnp.einsum("kdv,vjc->kdjc", kernel, onehot, preferred_element_type=jnp.float32)
    return bands.astype(jnp.bfloat16)


def stacked_rows(padded, height):
    return jnp.stack([padded[..., offset : offset + height, :] for offset in range(KER)], axis=-3)


def split_bf16(value):
    high = value.astype(jnp.bfloat16)
    low = (value - high.astype(jnp.float32)).astype(jnp.bfloat16)
    return high, low


def scatter_kernel(rows, columns, packet_ref, out_ref, acc_ref):
    acc_ref[...] = jnp.zeros_like(acc_ref)
    steps = packet_ref.shape[1] // CHUNK

    def body(step, carry):
        start = pl.multiple_of(step * CHUNK, CHUNK)
        block = packet_ref[:, pl.ds(start, CHUNK)]
        row_of = ((block[0:1] + 0.5) * (1.0 / columns)).astype(jnp.int32)
        col_of = block[0:1].astype(jnp.int32) - row_of * columns
        row_hot = (lax.broadcasted_iota(jnp.int32, (rows, CHUNK), 0) == row_of).astype(
            jnp.bfloat16
        )
        col_hot = (lax.broadcasted_iota(jnp.int32, (columns, CHUNK), 0) == col_of).astype(
            jnp.bfloat16
        )
        pieces = [split_bf16(block[field : field + 1]) for field in (1, 2, 3)]
        spread = jnp.concatenate(
            [col_hot * piece[half] for half in (0, 1) for piece in pieces], axis=0
        )
        acc_ref[...] += lax.dot_general(
            spread,
            row_hot,
            (((1,), (1,)), ((), ())),
            preferred_element_type=jnp.float32,
        )
        return carry

    lax.fori_loop(0, steps, body, 0)
    for field in range(3):
        out_ref[field] = (
            acc_ref[field * columns : (field + 1) * columns, :]
            + acc_ref[(field + 3) * columns : (field + 4) * columns, :]
        ).T


def deposit_sums(packet, rows, columns):
    count = packet.shape[1]
    flops = 2 * rows * 6 * columns * count
    return pl.pallas_call(
        functools.partial(scatter_kernel, rows, columns),
        out_shape=jax.ShapeDtypeStruct((3, rows, columns), jnp.float32),
        in_specs=[pl.BlockSpec(memory_space=pltpu.VMEM)],
        out_specs=pl.BlockSpec(memory_space=pltpu.VMEM),
        scratch_shapes=[pltpu.VMEM((6 * columns, rows), jnp.float32)],
        cost_estimate=pl.CostEstimate(
            flops=flops, bytes_accessed=packet.size * 4 + rows * 3 * columns * 4, transcendentals=0
        ),
    )(packet)


def correlate_kernel(x_ref, band_ref, out_ref, z_ref):
    bins, span, width = x_ref.shape
    height = out_ref.shape[2]
    x = x_ref[...].reshape(bins * span, width)
    for k in range(band_ref.shape[0]):
        total = jnp.zeros(out_ref.shape[1:], jnp.float32)
        for offset in range(band_ref.shape[1]):
            z_ref[...] = jnp.dot(
                x, band_ref[k, offset], preferred_element_type=jnp.float32
            ).reshape(z_ref.shape)
            total = total + z_ref[:, offset : offset + height, :]
        out_ref[k] = total


def correlate_forward(padded, bands, height):
    bins, span, width = padded.shape
    kinds, offsets, _, columns = bands.shape
    return pl.pallas_call(
        correlate_kernel,
        out_shape=jax.ShapeDtypeStruct((kinds, bins, height, columns), jnp.float32),
        in_specs=[pl.BlockSpec(memory_space=pltpu.VMEM)] * 2,
        out_specs=pl.BlockSpec(memory_space=pltpu.VMEM),
        scratch_shapes=[pltpu.VMEM((bins, span, columns), jnp.float32)],
        cost_estimate=pl.CostEstimate(
            flops=2 * kinds * offsets * bins * span * width * columns,
            bytes_accessed=padded.size * 2 + bands.size * 2 + kinds * bins * height * columns * 4,
            transcendentals=0,
        ),
    )(padded, bands)


def per_device(
    latent,
    shell_sigma,
    lens_weight,
    shear_kernel,
    star_mask,
    gal_pix,
    gal_bin,
    gal_shape,
    gal_weight,
    gal_counts,
):
    height = latent.shape[1]
    width = latent.shape[2]
    shell_count = lax.axis_size("shell")
    columns = width // shell_count
    pixels = height * columns

    slot_index = lax.broadcasted_iota(jnp.int32, gal_pix.shape, 2)
    usable = slot_index < gal_counts[:, :, None]
    codes = jnp.where(usable, gal_bin * pixels + gal_pix, 0).astype(jnp.float32)
    weights = jnp.where(usable, gal_weight, 0.0)
    packet = jnp.concatenate(
        [codes[None], weights[None], weights[None] * gal_shape], axis=0
    )
    devices = packet.shape[1] * packet.shape[2]
    arrived = lax.all_to_all(
        packet.reshape(4, devices, -1), ("shell", "tile"), split_axis=1, concat_axis=1, tiled=True
    )
    sum_rows = 256
    sums = deposit_sums(arrived.reshape(4, -1), sum_rows, NBIN * pixels // sum_rows)
    sums = sums.reshape(3, NBIN, height, columns)
    weight_sum = sums[0]
    shape_sum = sums[1:]

    sigma = shell_sigma[:, None, None]
    growth = jnp.exp(sigma * latent - 0.5 * sigma * sigma)
    partial_bins = jnp.einsum(
        "bs,srw->brw",
        lens_weight,
        growth - 1.0,
        precision=lax.Precision.HIGHEST,
        preferred_element_type=jnp.float32,
    )
    wide = jnp.pad(partial_bins, ((0, 0), (0, 0), (HALF, HALF)))
    windows = jnp.stack(
        [wide[:, :, owner * columns : owner * columns + columns + 2 * HALF] for owner in range(shell_count)]
    )
    me = lax.axis_index("shell")
    total = lax.dynamic_index_in_dim(windows, me, 0, keepdims=False)
    for shift in range(1, shell_count):
        outgoing = lax.dynamic_index_in_dim(windows, (me + shift) % shell_count, 0, keepdims=False)
        total = total + lax.ppermute(
            outgoing, "shell", [(i, (i + shift) % shell_count) for i in range(shell_count)]
        )
    bin_map = total.astype(jnp.bfloat16)
    padded = extended(bin_map, (("tile", 1),), HALF)
    forward_bands = build_bands(shear_kernel, columns)
    shear = correlate_forward(padded, forward_bands, height)
    shear_grad = shear * weight_sum[None] - shape_sum
    masked = (shear_grad * star_mask.astype(jnp.float32)).astype(jnp.bfloat16)
    rims = extended(masked, (("shell", 3), ("tile", 2)), HALF)
    back_bands = build_bands(jnp.flip(shear_kernel, (1, 2)), columns)
    bin_grad = jnp.einsum(
        "kbdrj,kdjc->brc",
        stacked_rows(rims, height),
        back_bands,
        preferred_element_type=jnp.float32,
    )
    full_grad = lax.all_gather(bin_grad, "shell", axis=2, tiled=True)
    mixed = jnp.einsum(
        "bs,brw->srw",
        lens_weight,
        full_grad,
        precision=lax.Precision.HIGHEST,
        preferred_element_type=jnp.float32,
    )
    return sigma * growth * mixed


def solution(mesh):
    return jax.shard_map(
        per_device,
        mesh=mesh,
        in_specs=(
            P("shell", "tile", None),
            P("shell"),
            P(None, "shell"),
            P(),
            P("tile", "shell"),
            P("shell", "tile", None),
            P("shell", "tile", None),
            P(None, "shell", "tile", None),
            P("shell", "tile", None),
            P("shell", "tile"),
        ),
        out_specs=P("shell", "tile", None),
        check_vma=False,
    )
```

```python
import functools

import jax
import jax.numpy as jnp
from jax import lax
from jax.experimental import pallas as pl
from jax.experimental.pallas import tpu as pltpu
from jax.sharding import PartitionSpec as P


NBIN = 5
KER = 33
HALF = 16
CHUNK = 8192


def extended(block, sides, width):
    for axis, dim in sides:
        count = lax.axis_size(axis)
        forward = [(i, i + 1) for i in range(count - 1)]
        backward = [(target, source) for source, target in forward]
        low = lax.ppermute(
            lax.slice_in_dim(block, block.shape[dim] - width, None, axis=dim), axis, forward
        )
        high = lax.ppermute(lax.slice_in_dim(block, 0, width, axis=dim), axis, backward)
        block = jnp.concatenate([low, block, high], axis=dim)
    return block


def neighbourhood(block, width):
    shells = lax.axis_size("shell")
    tiles = lax.axis_size("tile")
    rows, cols = block.shape[-2], block.shape[-1]
    row_parts = {-1: slice(rows - width, rows), 0: slice(0, rows), 1: slice(0, width)}
    col_parts = {-1: slice(cols - width, cols), 0: slice(0, cols), 1: slice(0, width)}
    pieces = {}
    for dt in (-1, 0, 1):
        for ds in (-1, 0, 1):
            part = block[..., row_parts[dt], col_parts[ds]]
            if dt == 0 and ds == 0:
                pieces[(dt, ds)] = part
                continue
            pairs = [
                (s * tiles + t, (s - ds) * tiles + (t - dt))
                for s in range(shells)
                for t in range(tiles)
                if 0 <= s - ds < shells and 0 <= t - dt < tiles
            ]
            pieces[(dt, ds)] = lax.ppermute(part, ("shell", "tile"), pairs)
    bands = [
        jnp.concatenate([pieces[(dt, -1)], pieces[(dt, 0)], pieces[(dt, 1)]], axis=-1)
        for dt in (-1, 0, 1)
    ]
    return jnp.concatenate(bands, axis=-2)


def build_bands(kernel, columns):
    span = columns + KER - 1
    grid_shape = (KER, span, columns)
    lagged = lax.broadcasted_iota(jnp.int32, grid_shape, 1) - lax.broadcasted_iota(
        jnp.int32, grid_shape, 2
    )
    onehot = (lagged == lax.broadcasted_iota(jnp.int32, grid_shape, 0)).astype(jnp.bfloat16)
    bands = jnp.einsum("kdv,vjc->kdjc", kernel, onehot, preferred_element_type=jnp.float32)
    return bands.astype(jnp.bfloat16)


def stacked_rows(padded, height):
    return jnp.stack([padded[..., offset : offset + height, :] for offset in range(KER)], axis=-3)


def split_bf16(value):
    high = value.astype(jnp.bfloat16)
    low = (value - high.astype(jnp.float32)).astype(jnp.bfloat16)
    return high, low


def scatter_kernel(rows, columns, packet_ref, out_ref, acc_ref):
    acc_ref[...] = jnp.zeros_like(acc_ref)
    steps = packet_ref.shape[1] // CHUNK

    def body(step, carry):
        start = pl.multiple_of(step * CHUNK, CHUNK)
        block = packet_ref[:, pl.ds(start, CHUNK)]
        row_of = ((block[0:1] + 0.5) * (1.0 / columns)).astype(jnp.int32)
        col_of = block[0:1].astype(jnp.int32) - row_of * columns
        row_hot = (lax.broadcasted_iota(jnp.int32, (rows, CHUNK), 0) == row_of).astype(
            jnp.bfloat16
        )
        col_hot = (lax.broadcasted_iota(jnp.int32, (columns, CHUNK), 0) == col_of).astype(
            jnp.bfloat16
        )
        pieces = [split_bf16(block[field : field + 1]) for field in (1, 2, 3)]
        spread = jnp.concatenate(
            [col_hot * piece[half] for half in (0, 1) for piece in pieces], axis=0
        )
        acc_ref[...] += lax.dot_general(
            spread,
            row_hot,
            (((1,), (1,)), ((), ())),
            preferred_element_type=jnp.float32,
        )
        return carry

    lax.fori_loop(0, steps, body, 0)
    for field in range(3):
        out_ref[field] = (
            acc_ref[field * columns : (field + 1) * columns, :]
            + acc_ref[(field + 3) * columns : (field + 4) * columns, :]
        ).T


def deposit_sums(packet, rows, columns):
    count = packet.shape[1]
    flops = 2 * rows * 6 * columns * count
    return pl.pallas_call(
        functools.partial(scatter_kernel, rows, columns),
        out_shape=jax.ShapeDtypeStruct((3, rows, columns), jnp.float32),
        in_specs=[pl.BlockSpec(memory_space=pltpu.VMEM)],
        out_specs=pl.BlockSpec(memory_space=pltpu.VMEM),
        scratch_shapes=[pltpu.VMEM((6 * columns, rows), jnp.float32)],
        cost_estimate=pl.CostEstimate(
            flops=flops, bytes_accessed=packet.size * 4 + rows * 3 * columns * 4, transcendentals=0
        ),
    )(packet)


def correlate_kernel(x_ref, band_ref, out_ref, z_ref):
    bins, span, width = x_ref.shape
    height = out_ref.shape[2]
    x = x_ref[...].reshape(bins * span, width)
    for k in range(band_ref.shape[0]):
        total = jnp.zeros(out_ref.shape[1:], jnp.float32)
        for offset in range(band_ref.shape[1]):
            z_ref[...] = jnp.dot(
                x, band_ref[k, offset], preferred_element_type=jnp.float32
            ).reshape(z_ref.shape)
            total = total + z_ref[:, offset : offset + height, :]
        out_ref[k] = total


def correlate_forward(padded, bands, height):
    bins, span, width = padded.shape
    kinds, offsets, _, columns = bands.shape
    return pl.pallas_call(
        correlate_kernel,
        out_shape=jax.ShapeDtypeStruct((kinds, bins, height, columns), jnp.float32),
        in_specs=[pl.BlockSpec(memory_space=pltpu.VMEM)] * 2,
        out_specs=pl.BlockSpec(memory_space=pltpu.VMEM),
        scratch_shapes=[pltpu.VMEM((bins, span, columns), jnp.float32)],
        cost_estimate=pl.CostEstimate(
            flops=2 * kinds * offsets * bins * span * width * columns,
            bytes_accessed=padded.size * 2 + bands.size * 2 + kinds * bins * height * columns * 4,
            transcendentals=0,
        ),
    )(padded, bands)


def per_device(
    latent,
    shell_sigma,
    lens_weight,
    shear_kernel,
    star_mask,
    gal_pix,
    gal_bin,
    gal_shape,
    gal_weight,
    gal_counts,
):
    height = latent.shape[1]
    width = latent.shape[2]
    shell_count = lax.axis_size("shell")
    columns = width // shell_count
    pixels = height * columns

    slot_index = lax.broadcasted_iota(jnp.int32, gal_pix.shape, 2)
    usable = slot_index < gal_counts[:, :, None]
    codes = jnp.where(usable, gal_bin * pixels + gal_pix, 0).astype(jnp.float32)
    weights = jnp.where(usable, gal_weight, 0.0)
    packet = jnp.concatenate(
        [codes[None], weights[None], weights[None] * gal_shape], axis=0
    )
    devices = packet.shape[1] * packet.shape[2]
    arrived = lax.all_to_all(
        packet.reshape(4, devices, -1), ("shell", "tile"), split_axis=1, concat_axis=1, tiled=True
    )
    sum_rows = 256
    sums = deposit_sums(arrived.reshape(4, -1), sum_rows, NBIN * pixels // sum_rows)
    sums = sums.reshape(3, NBIN, height, columns)
    weight_sum = sums[0]
    shape_sum = sums[1:]

    sigma = shell_sigma[:, None, None]
    growth = jnp.exp(sigma * latent - 0.5 * sigma * sigma)
    shells = latent.shape[0]
    partial_bins = jnp.dot(
        lens_weight,
        (growth - 1.0).reshape(shells, height * width),
        precision=lax.Precision.HIGHEST,
        preferred_element_type=jnp.float32,
    ).reshape(NBIN, height, width)
    wide = jnp.pad(partial_bins, ((0, 0), (0, 0), (HALF, HALF)))
    windows = jnp.stack(
        [wide[:, :, owner * columns : owner * columns + columns + 2 * HALF] for owner in range(shell_count)]
    )
    me = lax.axis_index("shell")
    total = lax.dynamic_index_in_dim(windows, me, 0, keepdims=False)
    for shift in range(1, shell_count):
        outgoing = lax.dynamic_index_in_dim(windows, (me + shift) % shell_count, 0, keepdims=False)
        total = total + lax.ppermute(
            outgoing, "shell", [(i, (i + shift) % shell_count) for i in range(shell_count)]
        )
    bin_map = total.astype(jnp.bfloat16)
    padded = extended(bin_map, (("tile", 1),), HALF)
    forward_bands = build_bands(shear_kernel, columns)
    shear = correlate_forward(padded, forward_bands, height)
    shear_grad = shear * weight_sum[None] - shape_sum
    masked = (shear_grad * star_mask.astype(jnp.float32)).astype(jnp.bfloat16)
    rims = neighbourhood(masked, HALF)
    back_bands = build_bands(jnp.flip(shear_kernel, (1, 2)), columns)
    bin_grad = jnp.einsum(
        "kbdrj,kdjc->brc",
        stacked_rows(rims, height),
        back_bands,
        preferred_element_type=jnp.float32,
    )
    received = [bin_grad]
    for shift in range(1, shell_count):
        received.append(
            lax.ppermute(
                bin_grad, "shell", [(i, (i + shift) % shell_count) for i in range(shell_count)]
            )
        )
    by_offset = jnp.stack([received[(-j) % shell_count] for j in range(shell_count)])
    twice = jnp.concatenate([by_offset, by_offset], axis=0)
    blocks = lax.dynamic_slice_in_dim(twice, (shell_count - me) % shell_count, shell_count, 0)
    full_grad = jnp.transpose(blocks, (1, 2, 0, 3)).reshape(NBIN, height * width)
    mixed = jnp.dot(
        lens_weight.T,
        full_grad,
        precision=lax.Precision.HIGHEST,
        preferred_element_type=jnp.float32,
    ).reshape(shells, height, width)
    return sigma * growth * mixed


def solution(mesh):
    return jax.shard_map(
        per_device,
        mesh=mesh,
        in_specs=(
            P("shell", "tile", None),
            P("shell"),
            P(None, "shell"),
            P(),
            P("tile", "shell"),
            P("shell", "tile", None),
            P("shell", "tile", None),
            P(None, "shell", "tile", None),
            P("shell", "tile", None),
            P("shell", "tile"),
        ),
        out_specs=P("shell", "tile", None),
        check_vma=False,
    )
```

```python
import functools

import jax
import jax.numpy as jnp
from jax import lax
from jax.experimental import pallas as pl
from jax.experimental.pallas import tpu as pltpu
from jax.sharding import PartitionSpec as P


NBIN = 5
KER = 33
HALF = 16
CHUNK = 8192


def extended(block, sides, width):
    for axis, dim in sides:
        count = lax.axis_size(axis)
        forward = [(i, i + 1) for i in range(count - 1)]
        backward = [(target, source) for source, target in forward]
        low = lax.ppermute(
            lax.slice_in_dim(block, block.shape[dim] - width, None, axis=dim), axis, forward
        )
        high = lax.ppermute(lax.slice_in_dim(block, 0, width, axis=dim), axis, backward)
        block = jnp.concatenate([low, block, high], axis=dim)
    return block


def build_bands(kernel, columns):
    span = columns + KER - 1
    grid_shape = (KER, span, columns)
    lagged = lax.broadcasted_iota(jnp.int32, grid_shape, 1) - lax.broadcasted_iota(
        jnp.int32, grid_shape, 2
    )
    onehot = (lagged == lax.broadcasted_iota(jnp.int32, grid_shape, 0)).astype(jnp.bfloat16)
    bands = jnp.einsum("kdv,vjc->kdjc", kernel, onehot, preferred_element_type=jnp.float32)
    return bands.astype(jnp.bfloat16)


def stacked_rows(padded, height):
    return jnp.stack([padded[..., offset : offset + height, :] for offset in range(KER)], axis=-3)


def split_bf16(value):
    high = value.astype(jnp.bfloat16)
    low = (value - high.astype(jnp.float32)).astype(jnp.bfloat16)
    return high, low


def scatter_kernel(rows, columns, packet_ref, out_ref, acc_ref):
    acc_ref[...] = jnp.zeros_like(acc_ref)
    steps = packet_ref.shape[1] // CHUNK

    def body(step, carry):
        start = pl.multiple_of(step * CHUNK, CHUNK)
        block = packet_ref[:, pl.ds(start, CHUNK)]
        row_of = ((block[0:1] + 0.5) * (1.0 / columns)).astype(jnp.int32)
        col_of = block[0:1].astype(jnp.int32) - row_of * columns
        row_hot = (lax.broadcasted_iota(jnp.int32, (rows, CHUNK), 0) == row_of).astype(
            jnp.bfloat16
        )
        col_hot = (lax.broadcasted_iota(jnp.int32, (columns, CHUNK), 0) == col_of).astype(
            jnp.bfloat16
        )
        pieces = [split_bf16(block[field : field + 1]) for field in (1, 2, 3)]
        spread = jnp.concatenate(
            [col_hot * piece[half] for half in (0, 1) for piece in pieces], axis=0
        )
        acc_ref[...] += lax.dot_general(
            spread,
            row_hot,
            (((1,), (1,)), ((), ())),
            preferred_element_type=jnp.float32,
        )
        return carry

    lax.fori_loop(0, steps, body, 0)
    for field in range(3):
        out_ref[field] = (
            acc_ref[field * columns : (field + 1) * columns, :]
            + acc_ref[(field + 3) * columns : (field + 4) * columns, :]
        ).T


def deposit_sums(packet, rows, columns):
    count = packet.shape[1]
    flops = 2 * rows * 6 * columns * count
    return pl.pallas_call(
        functools.partial(scatter_kernel, rows, columns),
        out_shape=jax.ShapeDtypeStruct((3, rows, columns), jnp.float32),
        in_specs=[pl.BlockSpec(memory_space=pltpu.VMEM)],
        out_specs=pl.BlockSpec(memory_space=pltpu.VMEM),
        scratch_shapes=[pltpu.VMEM((6 * columns, rows), jnp.float32)],
        cost_estimate=pl.CostEstimate(
            flops=flops, bytes_accessed=packet.size * 4 + rows * 3 * columns * 4, transcendentals=0
        ),
    )(packet)


def correlate_kernel(x_ref, band_ref, out_ref, z_ref):
    bins, span, width = x_ref.shape
    height = out_ref.shape[2]
    x = x_ref[...].reshape(bins * span, width)
    for k in range(band_ref.shape[0]):
        total = jnp.zeros(out_ref.shape[1:], jnp.float32)
        for offset in range(band_ref.shape[1]):
            z_ref[...] = jnp.dot(
                x, band_ref[k, offset], preferred_element_type=jnp.float32
            ).reshape(z_ref.shape)
            total = total + z_ref[:, offset : offset + height, :]
        out_ref[k] = total


def correlate_forward(padded, bands, height):
    bins, span, width = padded.shape
    kinds, offsets, _, columns = bands.shape
    return pl.pallas_call(
        correlate_kernel,
        out_shape=jax.ShapeDtypeStruct((kinds, bins, height, columns), jnp.float32),
        in_specs=[pl.BlockSpec(memory_space=pltpu.VMEM)] * 2,
        out_specs=pl.BlockSpec(memory_space=pltpu.VMEM),
        scratch_shapes=[pltpu.VMEM((bins, span, columns), jnp.float32)],
        cost_estimate=pl.CostEstimate(
            flops=2 * kinds * offsets * bins * span * width * columns,
            bytes_accessed=padded.size * 2 + bands.size * 2 + kinds * bins * height * columns * 4,
            transcendentals=0,
        ),
    )(padded, bands)


def per_device(
    latent,
    shell_sigma,
    lens_weight,
    shear_kernel,
    star_mask,
    gal_pix,
    gal_bin,
    gal_shape,
    gal_weight,
    gal_counts,
):
    height = latent.shape[1]
    width = latent.shape[2]
    shell_count = lax.axis_size("shell")
    columns = width // shell_count
    pixels = height * columns

    slot_index = lax.broadcasted_iota(jnp.int32, gal_pix.shape, 2)
    usable = slot_index < gal_counts[:, :, None]
    codes = jnp.where(usable, gal_bin * pixels + gal_pix, 0).astype(jnp.float32)
    weights = jnp.where(usable, gal_weight, 0.0)
    packet = jnp.concatenate(
        [codes[None], weights[None], weights[None] * gal_shape], axis=0
    )
    devices = packet.shape[1] * packet.shape[2]
    arrived = lax.all_to_all(
        packet.reshape(4, devices, -1), ("shell", "tile"), split_axis=1, concat_axis=1, tiled=True
    )
    sum_rows = 256
    sums = deposit_sums(arrived.reshape(4, -1), sum_rows, NBIN * pixels // sum_rows)
    sums = sums.reshape(3, NBIN, height, columns)
    weight_sum = sums[0]
    shape_sum = sums[1:]

    sigma = shell_sigma[:, None, None]
    growth = jnp.exp(sigma * latent - 0.5 * sigma * sigma)
    shells = latent.shape[0]
    partial_bins = jnp.dot(
    lens_weight,
        (growth - 1.0).reshape(shells, height * width),
        precision=lax.Precision.HIGHEST,
        preferred_element_type=jnp.float32,
    ).reshape(NBIN, height, width)
    wide = jnp.pad(partial_bins, ((0, 0), (0, 0), (HALF, HALF)))
    windows = jnp.stack(
        [wide[:, :, owner * columns : owner * columns + columns + 2 * HALF] for owner in range(shell_count)]
    )
    me = lax.axis_index("shell")
    total = lax.dynamic_index_in_dim(windows, me, 0, keepdims=False)
    for shift in range(1, shell_count):
        outgoing = lax.dynamic_index_in_dim(windows, (me + shift) % shell_count, 0, keepdims=False)
        total = total + lax.ppermute(
            outgoing, "shell", [(i, (i + shift) % shell_count) for i in range(shell_count)]
        )
    bin_map = total.astype(jnp.bfloat16)
    padded = extended(bin_map, (("tile", 1),), HALF)
    forward_bands = build_bands(shear_kernel, columns)
    shear = correlate_forward(padded, forward_bands, height)
    shear_grad = shear * weight_sum[None] - shape_sum
    masked = (shear_grad * star_mask.astype(jnp.float32)).astype(jnp.bfloat16)
    rims = extended(masked, (("shell", 3), ("tile", 2)), HALF)
    back_bands = build_bands(jnp.flip(shear_kernel, (1, 2)), columns)
    bin_grad = jnp.einsum(
        "kbdrj,kdjc->brc",
        stacked_rows(rims, height),
        back_bands,
        preferred_element_type=jnp.float32,
    )
    received = [bin_grad]
    for shift in range(1, shell_count):
        received.append(
            lax.ppermute(
                bin_grad, "shell", [(i, (i + shift) % shell_count) for i in range(shell_count)]
            )
        )
    by_offset = jnp.stack([received[(-j) % shell_count] for j in range(shell_count)])
    twice = jnp.concatenate([by_offset, by_offset], axis=0)
    blocks = lax.dynamic_slice_in_dim(twice, (shell_count - me) % shell_count, shell_count, 0)
    full_grad = jnp.transpose(blocks, (1, 2, 0, 3)).reshape(NBIN, height * width)
    mixed = jnp.dot(
        lens_weight.T,
        full_grad,
        precision=lax.Precision.HIGHEST,
        preferred_element_type=jnp.float32,
    ).reshape(shells, height, width)
    return sigma * growth * mixed


def solution(mesh):
    return jax.shard_map(
        per_device,
        mesh=mesh,
        in_specs=(
            P("shell", "tile", None),
            P("shell"),
            P(None, "shell"),
            P(),
            P("tile", "shell"),
            P("shell", "tile", None),
            P("shell", "tile", None),
            P(None, "shell", "tile", None),
            P("shell", "tile", None),
            P("shell", "tile"),
        ),
        out_specs=P("shell", "tile", None),
        check_vma=False,
    )
```

```python
import functools

import jax
import jax.numpy as jnp
from jax import lax
from jax.experimental import pallas as pl
from jax.experimental.pallas import tpu as pltpu
from jax.sharding import PartitionSpec as P


NBIN = 5
KER = 33
HALF = 16
CHUNK = 8192


def extended(block, sides, width):
    for axis, dim in sides:
        count = lax.axis_size(axis)
        forward = [(i, i + 1) for i in range(count - 1)]
        backward = [(target, source) for source, target in forward]
        low = lax.ppermute(
            lax.slice_in_dim(block, block.shape[dim] - width, None, axis=dim), axis, forward
        )
        high = lax.ppermute(lax.slice_in_dim(block, 0, width, axis=dim), axis, backward)
        block = jnp.concatenate([low, block, high], axis=dim)
    return block


def build_bands(kernel, columns):
    span = columns + KER - 1
    grid_shape = (KER, span, columns)
    lagged = lax.broadcasted_iota(jnp.int32, grid_shape, 1) - lax.broadcasted_iota(
        jnp.int32, grid_shape, 2
    )
    onehot = (lagged == lax.broadcasted_iota(jnp.int32, grid_shape, 0)).astype(jnp.bfloat16)
    bands = jnp.einsum("kdv,vjc->kdjc", kernel, onehot, preferred_element_type=jnp.float32)
    return bands.astype(jnp.bfloat16)


def stacked_rows(padded, height):
    return jnp.stack([padded[..., offset : offset + height, :] for offset in range(KER)], axis=-3)


def split_bf16(value):
    high = value.astype(jnp.bfloat16)
    low = (value - high.astype(jnp.float32)).astype(jnp.bfloat16)
    return high, low


def scatter_kernel(rows, columns, packet_ref, out_ref, acc_ref):
    acc_ref[...] = jnp.zeros_like(acc_ref)
    steps = packet_ref.shape[1] // CHUNK

    def body(step, carry):
        start = pl.multiple_of(step * CHUNK, CHUNK)
        block = packet_ref[:, pl.ds(start, CHUNK)]
        row_of = ((block[0:1] + 0.5) * (1.0 / columns)).astype(jnp.int32)
        col_of = block[0:1].astype(jnp.int32) - row_of * columns
        row_hot = (lax.broadcasted_iota(jnp.int32, (rows, CHUNK), 0) == row_of).astype(
            jnp.bfloat16
        )
        col_hot = (lax.broadcasted_iota(jnp.int32, (columns, CHUNK), 0) == col_of).astype(
            jnp.bfloat16
        )
        pieces = [split_bf16(block[field : field + 1]) for field in (1, 2, 3)]
        spread = jnp.concatenate(
            [col_hot * piece[half] for half in (0, 1) for piece in pieces], axis=0
        )
        acc_ref[...] += lax.dot_general(
            spread,
            row_hot,
            (((1,), (1,)), ((), ())),
            preferred_element_type=jnp.float32,
        )
        return carry

    lax.fori_loop(0, steps, body, 0)
    for field in range(3):
        out_ref[field] = (
            acc_ref[field * columns : (field + 1) * columns, :]
            + acc_ref[(field + 3) * columns : (field + 4) * columns, :]
        ).T


def deposit_sums(packet, rows, columns):
    count = packet.shape[1]
    flops = 2 * rows * 6 * columns * count
    return pl.pallas_call(
        functools.partial(scatter_kernel, rows, columns),
        out_shape=jax.ShapeDtypeStruct((3, rows, columns), jnp.float32),
        in_specs=[pl.BlockSpec(memory_space=pltpu.VMEM)],
        out_specs=pl.BlockSpec(memory_space=pltpu.VMEM),
        scratch_shapes=[pltpu.VMEM((6 * columns, rows), jnp.float32)],
        cost_estimate=pl.CostEstimate(
            flops=flops, bytes_accessed=packet.size * 4 + rows * 3 * columns * 4, transcendentals=0
        ),
    )(packet)


def correlate_kernel(x_ref, band_ref, out_ref, z_ref):
    bins, span, width = x_ref.shape
    height = out_ref.shape[2]
    x = x_ref[...].reshape(bins * span, width)
    for k in range(band_ref.shape[0]):
        total = jnp.zeros(out_ref.shape[1:], jnp.float32)
        for offset in range(band_ref.shape[1]):
            z_ref[...] = jnp.dot(
                x, band_ref[k, offset], preferred_element_type=jnp.float32
            ).reshape(z_ref.shape)
            total = total + z_ref[:, offset : offset + height, :]
        out_ref[k] = total


def correlate_forward(padded, bands, height):
    bins, span, width = padded.shape
    kinds, offsets, _, columns = bands.shape
    return pl.pallas_call(
        correlate_kernel,
        out_shape=jax.ShapeDtypeStruct((kinds, bins, height, columns), jnp.float32),
        in_specs=[pl.BlockSpec(memory_space=pltpu.VMEM)] * 2,
        out_specs=pl.BlockSpec(memory_space=pltpu.VMEM),
        scratch_shapes=[pltpu.VMEM((bins, span, columns), jnp.float32)],
        cost_estimate=pl.CostEstimate(
            flops=2 * kinds * offsets * bins * span * width * columns,
            bytes_accessed=padded.size * 2 + bands.size * 2 + kinds * bins * height * columns * 4,
            transcendentals=0,
        ),
    )(padded, bands)


def per_device(
    latent,
    shell_sigma,
    lens_weight,
    shear_kernel,
    star_mask,
    gal_pix,
    gal_bin,
    gal_shape,
    gal_weight,
    gal_counts,
):
    height = latent.shape[1]
    width = latent.shape[2]
    shell_count = lax.axis_size("shell")
    columns = width // shell_count
    pixels = height * columns

    slot_index = lax.broadcasted_iota(jnp.int32, gal_pix.shape, 2)
    usable = slot_index < gal_counts[:, :, None]
    codes = jnp.where(usable, gal_bin * pixels + gal_pix, 0).astype(jnp.float32)
    weights = jnp.where(usable, gal_weight, 0.0)
    packet = jnp.concatenate(
        [codes[None], weights[None], weights[None] * gal_shape], axis=0
    )
    devices = packet.shape[1] * packet.shape[2]
    arrived = lax.all_to_all(
        packet.reshape(4, devices, -1), ("shell", "tile"), split_axis=1, concat_axis=1, tiled=True
    )
    sum_rows = 256
    sums = deposit_sums(arrived.reshape(4, -1), sum_rows, NBIN * pixels // sum_rows)
    sums = lax.optimization_barrier(sums.reshape(3, NBIN, height, columns))
    weight_sum = sums[0]
    shape_sum = sums[1:]

    sigma = shell_sigma[:, None, None]
    growth = jnp.exp(sigma * latent - 0.5 * sigma * sigma)
    partial_bins = jnp.sum(lens_weight[:, :, None, None] * (growth - 1.0)[None], axis=1)
    wide = jnp.pad(partial_bins, ((0, 0), (0, 0), (HALF, HALF)))
    windows = jnp.stack(
        [wide[:, :, owner * columns : owner * columns + columns + 2 * HALF] for owner in range(shell_count)]
    )
    me = lax.axis_index("shell")
    total = lax.dynamic_index_in_dim(windows, me, 0, keepdims=False)
    for shift in range(1, shell_count):
        outgoing = lax.dynamic_index_in_dim(windows, (me + shift) % shell_count, 0, keepdims=False)
        total = total + lax.ppermute(
            outgoing, "shell", [(i, (i + shift) % shell_count) for i in range(shell_count)]
        )
    bin_map = total.astype(jnp.bfloat16)
    padded = extended(bin_map, (("tile", 1),), HALF)
    forward_bands = build_bands(shear_kernel, columns)
    shear = correlate_forward(padded, forward_bands, height)
    shear_grad = shear * weight_sum[None] - shape_sum
    masked = (shear_grad * star_mask.astype(jnp.float32)).astype(jnp.bfloat16)
    rims = extended(masked, (("tile", 2), ("shell", 3)), HALF)
    back_bands = build_bands(jnp.flip(shear_kernel, (1, 2)), columns)
    bin_grad = jnp.einsum(
        "kbdrj,kdjc->brc",
        stacked_rows(rims, height),
        back_bands,
        preferred_element_type=jnp.float32,
    )
    received = [bin_grad]
    for shift in range(1, shell_count):
        received.append(
            lax.ppermute(
                bin_grad, "shell", [(i, (i + shift) % shell_count) for i in range(shell_count)]
            )
        )
    by_offset = jnp.stack([received[(-j) % shell_count] for j in range(shell_count)])
    twice = jnp.concatenate([by_offset, by_offset], axis=0)
    blocks = lax.dynamic_slice_in_dim(twice, (shell_count - me) % shell_count, shell_count, 0)
    full_grad = jnp.transpose(blocks, (1, 2, 0, 3)).reshape(NBIN, height, width)
    mixed = jnp.sum(lens_weight.T[:, :, None, None] * full_grad[None], axis=1)
    return sigma * growth * mixed


def solution(mesh):
    return jax.shard_map(
        per_device,
        mesh=mesh,
        in_specs=(
            P("shell", "tile", None),
            P("shell"),
            P(None, "shell"),
            P(),
            P("tile", "shell"),
            P("shell", "tile", None),
            P("shell", "tile", None),
            P(None, "shell", "tile", None),
            P("shell", "tile", None),
            P("shell", "tile"),
        ),
        out_specs=P("shell", "tile", None),
        check_vma=False,
    )
```

```python
import functools

import jax
import jax.numpy as jnp
from jax import lax
from jax.experimental import pallas as pl
from jax.experimental.pallas import tpu as pltpu
from jax.sharding import PartitionSpec as P


NBIN = 5
KER = 33
HALF = 16
CHUNK = 8192


def extended(block, sides, width):
    for axis, dim in sides:
        count = lax.axis_size(axis)
        forward = [(i, i + 1) for i in range(count - 1)]
        backward = [(target, source) for source, target in forward]
        low = lax.ppermute(
            lax.slice_in_dim(block, block.shape[dim] - width, None, axis=dim), axis, forward
        )
        high = lax.ppermute(lax.slice_in_dim(block, 0, width, axis=dim), axis, backward)
        block = jnp.concatenate([low, block, high], axis=dim)
    return block


def build_bands(kernel, columns):
    span = columns + KER - 1
    grid_shape = (KER, span, columns)
    lagged = lax.broadcasted_iota(jnp.int32, grid_shape, 1) - lax.broadcasted_iota(
        jnp.int32, grid_shape, 2
    )
    onehot = (lagged == lax.broadcasted_iota(jnp.int32, grid_shape, 0)).astype(jnp.bfloat16)
    bands = jnp.einsum("kdv,vjc->kdjc", kernel, onehot, preferred_element_type=jnp.float32)
    return bands.astype(jnp.bfloat16)


def stacked_rows(padded, height):
    return jnp.stack([padded[..., offset : offset + height, :] for offset in range(KER)], axis=-3)


def split_bf16(value):
    high = value.astype(jnp.bfloat16)
    low = (value - high.astype(jnp.float32)).astype(jnp.bfloat16)
    return high, low


def scatter_kernel(rows, columns, packet_ref, out_ref, acc_ref):
    acc_ref[...] = jnp.zeros_like(acc_ref)
    steps = packet_ref.shape[1] // CHUNK

    def body(step, carry):
        start = pl.multiple_of(step * CHUNK, CHUNK)
        block = packet_ref[:, pl.ds(start, CHUNK)]
        row_of = ((block[0:1] + 0.5) * (1.0 / columns)).astype(jnp.int32)
        col_of = block[0:1].astype(jnp.int32) - row_of * columns
        row_hot = (lax.broadcasted_iota(jnp.int32, (rows, CHUNK), 0) == row_of).astype(
            jnp.bfloat16
        )
        col_hot = (lax.broadcasted_iota(jnp.int32, (columns, CHUNK), 0) == col_of).astype(
            jnp.bfloat16
        )
        pieces = [split_bf16(block[field : field + 1]) for field in (1, 2, 3)]
        spread = jnp.concatenate(
            [col_hot * piece[half] for half in (0, 1) for piece in pieces], axis=0
        )
        acc_ref[...] += lax.dot_general(
            spread,
            row_hot,
            (((1,), (1,)), ((), ())),
            preferred_element_type=jnp.float32,
        )
        return carry

    lax.fori_loop(0, steps, body, 0)
    for field in range(3):
        out_ref[field] = (
            acc_ref[field * columns : (field + 1) * columns, :]
            + acc_ref[(field + 3) * columns : (field + 4) * columns, :]
        ).T


def deposit_sums(packet, rows, columns):
    count = packet.shape[1]
    flops = 2 * rows * 6 * columns * count
    return pl.pallas_call(
        functools.partial(scatter_kernel, rows, columns),
        out_shape=jax.ShapeDtypeStruct((3, rows, columns), jnp.float32),
        in_specs=[pl.BlockSpec(memory_space=pltpu.VMEM)],
        out_specs=pl.BlockSpec(memory_space=pltpu.VMEM),
        scratch_shapes=[pltpu.VMEM((6 * columns, rows), jnp.float32)],
        cost_estimate=pl.CostEstimate(
            flops=flops, bytes_accessed=packet.size * 4 + rows * 3 * columns * 4, transcendentals=0
        ),
    )(packet)


def correlate_kernel(x_ref, band_ref, out_ref, z_ref):
    bins, span, width = x_ref.shape
    height = out_ref.shape[2]
    x = x_ref[...].reshape(bins * span, width)
    for k in range(band_ref.shape[0]):
        total = jnp.zeros(out_ref.shape[1:], jnp.float32)
        for offset in range(band_ref.shape[1]):
            z_ref[...] = jnp.dot(
                x, band_ref[k, offset], preferred_element_type=jnp.float32
            ).reshape(z_ref.shape)
            total = total + z_ref[:, offset : offset + height, :]
        out_ref[k] = total


def correlate_forward(padded, bands, height):
    bins, span, width = padded.shape
    kinds, offsets, _, columns = bands.shape
    return pl.pallas_call(
        correlate_kernel,
        out_shape=jax.ShapeDtypeStruct((kinds, bins, height, columns), jnp.float32),
        in_specs=[pl.BlockSpec(memory_space=pltpu.VMEM)] * 2,
        out_specs=pl.BlockSpec(memory_space=pltpu.VMEM),
        scratch_shapes=[pltpu.VMEM((bins, span, columns), jnp.float32)],
        cost_estimate=pl.CostEstimate(
            flops=2 * kinds * offsets * bins * span * width * columns,
            bytes_accessed=padded.size * 2 + bands.size * 2 + kinds * bins * height * columns * 4,
            transcendentals=0,
        ),
    )(padded, bands)


def per_device(
    latent,
    shell_sigma,
    lens_weight,
    shear_kernel,
    star_mask,
    gal_pix,
    gal_bin,
    gal_shape,
    gal_weight,
    gal_counts,
):
    height = latent.shape[1]
    width = latent.shape[2]
    shell_count = lax.axis_size("shell")
    columns = width // shell_count
    pixels = height * columns

    slot_index = lax.broadcasted_iota(jnp.int32, gal_pix.shape, 2)
    usable = slot_index < gal_counts[:, :, None]
    codes = jnp.where(usable, gal_bin * pixels + gal_pix, 0).astype(jnp.float32)
    weights = jnp.where(usable, gal_weight, 0.0)
    packet = jnp.concatenate(
        [codes[None], weights[None], weights[None] * gal_shape], axis=0
    )
    devices = packet.shape[1] * packet.shape[2]
    arrived = lax.all_to_all(
        packet.reshape(4, devices, -1), ("shell", "tile"), split_axis=1, concat_axis=1, tiled=True
    )
    sum_rows = 256
    sums = deposit_sums(arrived.reshape(4, -1), sum_rows, NBIN * pixels // sum_rows)
    sums = sums.reshape(3, NBIN, height, columns)
    weight_sum = sums[0]
    shape_sum = sums[1:]

    sigma = shell_sigma[:, None, None]
    exponent = sigma * latent - 0.5 * sigma * sigma
    growth = jnp.exp(exponent)
    partial_bins = jnp.sum(lens_weight[:, :, None, None] * (growth - 1.0)[None], axis=1)
    wide = jnp.pad(partial_bins, ((0, 0), (0, 0), (HALF, HALF)))
    windows = jnp.stack(
        [wide[:, :, owner * columns : owner * columns + columns + 2 * HALF] for owner in range(shell_count)]
    )
    me = lax.axis_index("shell")
    total = lax.dynamic_index_in_dim(windows, me, 0, keepdims=False)
    for shift in range(1, shell_count):
        outgoing = lax.dynamic_index_in_dim(windows, (me + shift) % shell_count, 0, keepdims=False)
        total = total + lax.ppermute(
            outgoing, "shell", [(i, (i + shift) % shell_count) for i in range(shell_count)]
        )
    bin_map = total.astype(jnp.bfloat16)
    padded = extended(bin_map, (("tile", 1),), HALF)
    forward_bands = build_bands(shear_kernel, columns)
    shear = correlate_forward(padded, forward_bands, height)
    shear_grad = shear * weight_sum[None] - shape_sum
    masked = (shear_grad * star_mask.astype(jnp.float32)).astype(jnp.bfloat16)
    rims = extended(masked, (("shell", 3), ("tile", 2)), HALF)
    back_bands = build_bands(jnp.flip(shear_kernel, (1, 2)), columns)
    bin_grad = jnp.einsum(
        "kbdrj,kdjc->brc",
        stacked_rows(rims, height),
        back_bands,
        preferred_element_type=jnp.float32,
    )
    received = [bin_grad]
    for shift in range(1, shell_count):
        received.append(
            lax.ppermute(
                bin_grad, "shell", [(i, (i + shift) % shell_count) for i in range(shell_count)]
            )
        )
    by_offset = jnp.stack([received[(-j) % shell_count] for j in range(shell_count)])
    twice = jnp.concatenate([by_offset, by_offset], axis=0)
    blocks = lax.dynamic_slice_in_dim(twice, (shell_count - me) % shell_count, shell_count, 0)
    full_grad = jnp.transpose(blocks, (1, 2, 0, 3)).reshape(NBIN, height, width)
    mixed = jnp.sum(lens_weight.T[:, :, None, None] * full_grad[None], axis=1)
    return jnp.exp(exponent + jnp.log(sigma)) * mixed


def solution(mesh):
    return jax.shard_map(
        per_device,
        mesh=mesh,
        in_specs=(
            P("shell", "tile", None),
            P("shell"),
            P(None, "shell"),
            P(),
            P("tile", "shell"),
            P("shell", "tile", None),
            P("shell", "tile", None),
            P(None, "shell", "tile", None),
            P("shell", "tile", None),
            P("shell", "tile"),
        ),
        out_specs=P("shell", "tile", None),
        check_vma=False,
    )
```

```python
import functools

import jax
import jax.numpy as jnp
from jax import lax
from jax.experimental import pallas as pl
from jax.experimental.pallas import tpu as pltpu
from jax.sharding import PartitionSpec as P


NBIN = 5
KER = 33
HALF = 16
CHUNK = 32768


def extended(block, sides, width):
    for axis, dim in sides:
        count = lax.axis_size(axis)
        forward = [(i, i + 1) for i in range(count - 1)]
        backward = [(target, source) for source, target in forward]
        low = lax.ppermute(
            lax.slice_in_dim(block, block.shape[dim] - width, None, axis=dim), axis, forward
        )
        high = lax.ppermute(lax.slice_in_dim(block, 0, width, axis=dim), axis, backward)
        block = jnp.concatenate([low, block, high], axis=dim)
    return block


def build_bands(kernel, columns):
    span = columns + KER - 1
    grid_shape = (KER, span, columns)
    lagged = lax.broadcasted_iota(jnp.int32, grid_shape, 1) - lax.broadcasted_iota(
        jnp.int32, grid_shape, 2
    )
    onehot = (lagged == lax.broadcasted_iota(jnp.int32, grid_shape, 0)).astype(jnp.bfloat16)
    bands = jnp.einsum("kdv,vjc->kdjc", kernel, onehot, preferred_element_type=jnp.float32)
    return bands.astype(jnp.bfloat16)


def stacked_rows(padded, height):
    return jnp.stack([padded[..., offset : offset + height, :] for offset in range(KER)], axis=-3)


def split_bf16(value):
    high = value.astype(jnp.bfloat16)
    low = (value - high.astype(jnp.float32)).astype(jnp.bfloat16)
    return high, low


def scatter_kernel(rows, columns, packet_ref, out_ref, acc_ref):
    acc_ref[...] = jnp.zeros_like(acc_ref)
    steps = packet_ref.shape[1] // CHUNK

    def body(step, carry):
        start = pl.multiple_of(step * CHUNK, CHUNK)
        block = packet_ref[:, pl.ds(start, CHUNK)]
        row_of = ((block[0:1] + 0.5) * (1.0 / columns)).astype(jnp.int32)
        col_of = block[0:1].astype(jnp.int32) - row_of * columns
        row_hot = (lax.broadcasted_iota(jnp.int32, (rows, CHUNK), 0) == row_of).astype(
            jnp.bfloat16
        )
        col_hot = (lax.broadcasted_iota(jnp.int32, (columns, CHUNK), 0) == col_of).astype(
            jnp.bfloat16
        )
        pieces = [split_bf16(block[field : field + 1]) for field in (1, 2, 3)]
        spread = jnp.concatenate(
            [col_hot * piece[half] for half in (0, 1) for piece in pieces], axis=0
        )
        acc_ref[...] += lax.dot_general(
            spread,
            row_hot,
            (((1,), (1,)), ((), ())),
            preferred_element_type=jnp.float32,
        )
        return carry

    lax.fori_loop(0, steps, body, 0)
    for field in range(3):
        out_ref[field] = (
            acc_ref[field * columns : (field + 1) * columns, :]
            + acc_ref[(field + 3) * columns : (field + 4) * columns, :]
        ).T


def deposit_sums(packet, rows, columns):
    count = packet.shape[1]
    flops = 2 * rows * 6 * columns * count
    return pl.pallas_call(
        functools.partial(scatter_kernel, rows, columns),
        out_shape=jax.ShapeDtypeStruct((3, rows, columns), jnp.float32),
        in_specs=[pl.BlockSpec(memory_space=pltpu.VMEM)],
        out_specs=pl.BlockSpec(memory_space=pltpu.VMEM),
        scratch_shapes=[pltpu.VMEM((6 * columns, rows), jnp.float32)],
        cost_estimate=pl.CostEstimate(
            flops=flops, bytes_accessed=packet.size * 4 + rows * 3 * columns * 4, transcendentals=0
        ),
    )(packet)


def correlate_kernel(x_ref, band_ref, out_ref, z_ref):
    bins, span, width = x_ref.shape
    height = out_ref.shape[2]
    x = x_ref[...].reshape(bins * span, width)
    for k in range(band_ref.shape[0]):
        total = jnp.zeros(out_ref.shape[1:], jnp.float32)
        for offset in range(band_ref.shape[1]):
            z_ref[...] = jnp.dot(
                x, band_ref[k, offset], preferred_element_type=jnp.float32
            ).reshape(z_ref.shape)
            total = total + z_ref[:, offset : offset + height, :]
        out_ref[k] = total


def correlate_forward(padded, bands, height):
    bins, span, width = padded.shape
    kinds, offsets, _, columns = bands.shape
    return pl.pallas_call(
        correlate_kernel,
        out_shape=jax.ShapeDtypeStruct((kinds, bins, height, columns), jnp.float32),
        in_specs=[pl.BlockSpec(memory_space=pltpu.VMEM)] * 2,
        out_specs=pl.BlockSpec(memory_space=pltpu.VMEM),
        scratch_shapes=[pltpu.VMEM((bins, span, columns), jnp.float32)],
        cost_estimate=pl.CostEstimate(
            flops=2 * kinds * offsets * bins * span * width * columns,
            bytes_accessed=padded.size * 2 + bands.size * 2 + kinds * bins * height * columns * 4,
            transcendentals=0,
        ),
    )(padded, bands)


def per_device(
    latent,
    shell_sigma,
    lens_weight,
    shear_kernel,
    star_mask,
    gal_pix,
    gal_bin,
    gal_shape,
    gal_weight,
    gal_counts,
):
    height = latent.shape[1]
    width = latent.shape[2]
    shell_count = lax.axis_size("shell")
    columns = width // shell_count
    pixels = height * columns

    slot_index = lax.broadcasted_iota(jnp.int32, gal_pix.shape, 2)
    usable = slot_index < gal_counts[:, :, None]
    codes = jnp.where(usable, gal_bin * pixels + gal_pix, 0).astype(jnp.float32)
    weights = jnp.where(usable, gal_weight, 0.0)
    packet = jnp.concatenate(
        [codes[None], weights[None], weights[None] * gal_shape], axis=0
    )
    devices = packet.shape[1] * packet.shape[2]
    arrived = lax.all_to_all(
        packet.reshape(4, devices, -1), ("shell", "tile"), split_axis=1, concat_axis=1, tiled=True
    )
    sum_rows = 256
    sums = deposit_sums(arrived.reshape(4, -1), sum_rows, NBIN * pixels // sum_rows)
    sums = sums.reshape(3, NBIN, height, columns)
    weight_sum = sums[0]
    shape_sum = sums[1:]

    sigma = shell_sigma[:, None, None]
    growth = jnp.exp(sigma * latent - 0.5 * sigma * sigma)
    partial_bins = jnp.sum(lens_weight[:, :, None, None] * (growth - 1.0)[None], axis=1)
    wide = jnp.pad(partial_bins, ((0, 0), (0, 0), (HALF, HALF)))
    windows = jnp.stack(
        [wide[:, :, owner * columns : owner * columns + columns + 2 * HALF] for owner in range(shell_count)]
    )
    me = lax.axis_index("shell")
    total = lax.dynamic_index_in_dim(windows, me, 0, keepdims=False)
    for shift in range(1, shell_count):
        outgoing = lax.dynamic_index_in_dim(windows, (me + shift) % shell_count, 0, keepdims=False)
        total = total + lax.ppermute(
            outgoing, "shell", [(i, (i + shift) % shell_count) for i in range(shell_count)]
        )
    bin_map = total.astype(jnp.bfloat16)
    padded = extended(bin_map, (("tile", 1),), HALF)
    forward_bands = build_bands(shear_kernel, columns)
    shear = correlate_forward(padded, forward_bands, height)
    shear_grad = shear * weight_sum[None] - shape_sum
    masked = (shear_grad * star_mask.astype(jnp.float32)).astype(jnp.bfloat16)
    rims = extended(masked, (("shell", 3), ("tile", 2)), HALF)
    back_bands = build_bands(jnp.flip(shear_kernel, (1, 2)), columns)
    bin_grad = jnp.einsum(
        "kbdrj,kdjc->brc",
        stacked_rows(rims, height),
        back_bands,
        preferred_element_type=jnp.float32,
    )
    received = [bin_grad]
    for shift in range(1, shell_count):
        received.append(
            lax.ppermute(
                bin_grad, "shell", [(i, (i + shift) % shell_count) for i in range(shell_count)]
            )
        )
    by_offset = jnp.stack([received[(-j) % shell_count] for j in range(shell_count)])
    twice = jnp.concatenate([by_offset, by_offset], axis=0)
    blocks = lax.dynamic_slice_in_dim(twice, (shell_count - me) % shell_count, shell_count, 0)
    full_grad = jnp.transpose(blocks, (1, 2, 0, 3)).reshape(NBIN, height, width)
    mixed = jnp.sum(lens_weight.T[:, :, None, None] * full_grad[None], axis=1)
    return sigma * growth * mixed


def solution(mesh):
    return jax.shard_map(
        per_device,
        mesh=mesh,
        in_specs=(
            P("shell", "tile", None),
            P("shell"),
            P(None, "shell"),
            P(),
            P("tile", "shell"),
            P("shell", "tile", None),
            P("shell", "tile", None),
            P(None, "shell", "tile", None),
            P("shell", "tile", None),
            P("shell", "tile"),
        ),
        out_specs=P("shell", "tile", None),
        check_vma=False,
    )
```

```python
import functools

import jax
import jax.numpy as jnp
from jax import lax
from jax.experimental import pallas as pl
from jax.experimental.pallas import tpu as pltpu
from jax.sharding import PartitionSpec as P


NBIN = 5
KER = 33
HALF = 16
CHUNK = 32768


def extended(block, sides, width):
    for axis, dim in sides:
        count = lax.axis_size(axis)
        forward = [(i, i + 1) for i in range(count - 1)]
        backward = [(target, source) for source, target in forward]
        low = lax.ppermute(
            lax.slice_in_dim(block, block.shape[dim] - width, None, axis=dim), axis, forward
        )
        high = lax.ppermute(lax.slice_in_dim(block, 0, width, axis=dim), axis, backward)
        block = jnp.concatenate([low, block, high], axis=dim)
    return block


def build_bands(kernel, columns):
    span = columns + KER - 1
    grid_shape = (KER, span, columns)
    lagged = lax.broadcasted_iota(jnp.int32, grid_shape, 1) - lax.broadcasted_iota(
        jnp.int32, grid_shape, 2
    )
    onehot = (lagged == lax.broadcasted_iota(jnp.int32, grid_shape, 0)).astype(jnp.bfloat16)
    bands = jnp.einsum("kdv,vjc->kdjc", kernel, onehot, preferred_element_type=jnp.float32)
    return bands.astype(jnp.bfloat16)


def stacked_rows(padded, height):
    return jnp.stack([padded[..., offset : offset + height, :] for offset in range(KER)], axis=-3)


def split_bf16(value):
    high = value.astype(jnp.bfloat16)
    low = (value - high.astype(jnp.float32)).astype(jnp.bfloat16)
    return high, low


def scatter_kernel(rows, columns, packet_ref, out_ref, acc_ref):
    acc_ref[...] = jnp.zeros_like(acc_ref)
    steps = packet_ref.shape[1] // CHUNK

    def body(step, carry):
        start = pl.multiple_of(step * CHUNK, CHUNK)
        block = packet_ref[:, pl.ds(start, CHUNK)]
        row_of = ((block[0:1] + 0.5) * (1.0 / columns)).astype(jnp.int32)
        col_of = block[0:1].astype(jnp.int32) - row_of * columns
        row_hot = (lax.broadcasted_iota(jnp.int32, (rows, CHUNK), 0) == row_of).astype(
            jnp.bfloat16
        )
        col_hot = (lax.broadcasted_iota(jnp.int32, (columns, CHUNK), 0) == col_of).astype(
            jnp.bfloat16
        )
        pieces = [split_bf16(block[field : field + 1]) for field in (1, 2, 3)]
        spread = jnp.concatenate(
            [col_hot * piece[half] for half in (0, 1) for piece in pieces], axis=0
        )
        acc_ref[...] += lax.dot_general(
            spread,
            row_hot,
            (((1,), (1,)), ((), ())),
            preferred_element_type=jnp.float32,
        )
        return carry

    lax.fori_loop(0, steps, body, 0)
    for field in range(3):
        out_ref[field] = (
            acc_ref[field * columns : (field + 1) * columns, :]
            + acc_ref[(field + 3) * columns : (field + 4) * columns, :]
        ).T


def deposit_sums(packet, rows, columns):
    count = packet.shape[1]
    flops = 2 * rows * 6 * columns * count
    return pl.pallas_call(
        functools.partial(scatter_kernel, rows, columns),
        out_shape=jax.ShapeDtypeStruct((3, rows, columns), jnp.float32),
        in_specs=[pl.BlockSpec(memory_space=pltpu.VMEM)],
        out_specs=pl.BlockSpec(memory_space=pltpu.VMEM),
        scratch_shapes=[pltpu.VMEM((6 * columns, rows), jnp.float32)],
        cost_estimate=pl.CostEstimate(
            flops=flops, bytes_accessed=packet.size * 4 + rows * 3 * columns * 4, transcendentals=0
        ),
    )(packet)


def correlate_kernel(x_ref, band_ref, out_ref, z_ref):
    bins, span, width = x_ref.shape
    height = out_ref.shape[2]
    x = x_ref[...].reshape(bins * span, width)
    for k in range(band_ref.shape[0]):
        total = jnp.zeros(out_ref.shape[1:], jnp.float32)
        for offset in range(band_ref.shape[1]):
            z_ref[...] = jnp.dot(
                x, band_ref[k, offset], preferred_element_type=jnp.float32
            ).reshape(z_ref.shape)
            total = total + z_ref[:, offset : offset + height, :]
        out_ref[k] = total


def correlate_forward(padded, bands, height):
    bins, span, width = padded.shape
    kinds, offsets, _, columns = bands.shape
    return pl.pallas_call(
        correlate_kernel,
        out_shape=jax.ShapeDtypeStruct((kinds, bins, height, columns), jnp.float32),
        in_specs=[pl.BlockSpec(memory_space=pltpu.VMEM)] * 2,
        out_specs=pl.BlockSpec(memory_space=pltpu.VMEM),
        scratch_shapes=[pltpu.VMEM((bins, span, columns), jnp.float32)],
        cost_estimate=pl.CostEstimate(
            flops=2 * kinds * offsets * bins * span * width * columns,
            bytes_accessed=padded.size * 2 + bands.size * 2 + kinds * bins * height * columns * 4,
            transcendentals=0,
        ),
    )(padded, bands)


def per_device(
    latent,
    shell_sigma,
    lens_weight,
    shear_kernel,
    star_mask,
    gal_pix,
    gal_bin,
    gal_shape,
    gal_weight,
    gal_counts,
):
    height = latent.shape[1]
    width = latent.shape[2]
    shell_count = lax.axis_size("shell")
    columns = width // shell_count
    pixels = height * columns

    slot_index = lax.broadcasted_iota(jnp.int32, gal_pix.shape, 2)
    usable = slot_index < gal_counts[:, :, None]
    codes = jnp.where(usable, gal_bin * pixels + gal_pix, 0).astype(jnp.float32)
    weights = jnp.where(usable, gal_weight, 0.0)
    packet = jnp.concatenate(
        [codes[None], weights[None], weights[None] * gal_shape], axis=0
    )
    devices = packet.shape[1] * packet.shape[2]
    arrived = lax.all_to_all(
        packet.reshape(4, devices, -1), ("shell", "tile"), split_axis=1, concat_axis=1, tiled=True
    )
    sum_rows = 256
    sums = deposit_sums(arrived.reshape(4, -1), sum_rows, NBIN * pixels // sum_rows)
    sums = sums.reshape(3, NBIN, height, columns)
    weight_sum = sums[0]
    shape_sum = sums[1:]

    sigma = shell_sigma[:, None, None]
    growth = jnp.exp(sigma * latent - 0.5 * sigma * sigma)
    partial_bins = jnp.sum(lens_weight[:, :, None, None] * (growth - 1.0)[None], axis=1)
    wide = jnp.pad(partial_bins, ((0, 0), (0, 0), (HALF, HALF)))
    windows = jnp.stack(
        [wide[:, :, owner * columns : owner * columns + columns + 2 * HALF] for owner in range(shell_count)]
    )
    me = lax.axis_index("shell")
    total = lax.dynamic_index_in_dim(windows, me, 0, keepdims=False)
    for shift in range(1, shell_count):
        outgoing = lax.dynamic_index_in_dim(windows, (me + shift) % shell_count, 0, keepdims=False)
        total = total + lax.ppermute(
            outgoing, "shell", [(i, (i + shift) % shell_count) for i in range(shell_count)]
        )
    bin_map = total.astype(jnp.bfloat16)
    padded = extended(bin_map, (("tile", 1),), HALF)
    forward_bands = build_bands(shear_kernel, columns)
    shear = correlate_forward(padded, forward_bands, height)
    shear_grad = shear * weight_sum[None] - shape_sum
    masked = (shear_grad * star_mask.astype(jnp.float32)).astype(jnp.bfloat16)
    rims = extended(masked, (("shell", 3), ("tile", 2)), HALF)
    back_bands = build_bands(jnp.flip(shear_kernel, (1, 2)), columns)
    bin_grad = jnp.einsum(
        "kbdrj,kdjc->brc",
        stacked_rows(rims, height),
        back_bands,
        preferred_element_type=jnp.float32,
    )
    full_grad = lax.all_gather(bin_grad, "shell", axis=2, tiled=True)
    mixed = jnp.sum(lens_weight.T[:, :, None, None] * full_grad[None], axis=1)
    return sigma * growth * mixed


def solution(mesh):
    return jax.shard_map(
        per_device,
        mesh=mesh,
        in_specs=(
            P("shell", "tile", None),
            P("shell"),
            P(None, "shell"),
            P(),
            P("tile", "shell"),
            P("shell", "tile", None),
            P("shell", "tile", None),
            P(None, "shell", "tile", None),
            P("shell", "tile", None),
            P("shell", "tile"),
        ),
        out_specs=P("shell", "tile", None),
        check_vma=False,
    )
```
